32 devices in a mesh: lat: 8 (over z, y), mode: 4 (over x, core).
Axes of the slice: x: 2, y: 2, z: 4, core: 2. Of those that a mesh axis runs over, the one named last changes fastest.
Arguments:
- earlier: bfloat16 [64, 32, 36864], P(None, ('lat', 'mode')), may hold values from -4 to 4
- panels: bfloat16 [2, 16, 32, 36864], P(None, 'mode', None, 'lat'), may hold values from -28 to 28
- further: bfloat16 [16, 32, 36864], P('mode', None, 'lat'), may hold values from -32 to 32
Outputs:
- new_basis: bfloat16 [2, 16, 32, 36864], P(None, None, ('lat', 'mode'))
- coarse: float32 [16, 32, 96], P(None, ('lat', 'mode'))
The draws below stay inside these ranges and needn't reach their ends.
All inputs are finite; a program needn't handle non-finite values.
Results may differ from the reference program's by a relative error of at most 0.0062.
Values may be sent and summed in bfloat16 or wider, within the bound.
No kernel may reach another device: no remote copies, remote signals or barrier semaphores. Data moves between devices by JAX's collectives and lax.ppermute only.
A program may use at most 64 MiB of HBM per device.

```python
import jax
import jax.numpy as jnp
from jax import lax

BLEN = 36864
P_SIZE = 16
NB = 64
PANELS = 2
NBLK = 32


def basis_rows(key):
    basis_key = jax.random.fold_in(key, 11)
    return jax.random.truncated_normal(basis_key, -4.0, 4.0, (NB, NBLK, BLEN), jnp.float32)


def column_scale(key):
    return jnp.exp(jax.random.uniform(jax.random.fold_in(key, 13), (NBLK, BLEN), jnp.float32, -1.15, 1.15))


def noise_part(key, index, scales):
    noise_key = jax.random.fold_in(key, 100 + index)
    return jax.random.truncated_normal(noise_key, -4.0, 4.0, (P_SIZE, NBLK, BLEN), jnp.float32) * scales


def picked_rows(key, basis, salt):
    picks = jax.random.randint(jax.random.fold_in(key, salt), (P_SIZE,), 0, NB)
    return basis[picks]


def draw_earlier(key, part):
    return basis_rows(key).astype(jnp.bfloat16)


def draw_panels(key, part):
    basis = basis_rows(key)
    scales = column_scale(key)
    stacked = []
    for panel_index in range(PANELS):
        vectors = picked_rows(key, basis, 200 + panel_index) - 0.7 * picked_rows(key, basis, 300 + panel_index)
        vectors = vectors + noise_part(key, panel_index, scales)
        if panel_index > 0:
            vectors = vectors + 0.6 * noise_part(key, panel_index - 1, scales)
        stacked.append(vectors)
    return jnp.stack(stacked, 0).astype(jnp.bfloat16)


def draw_further(key, part):
    basis = basis_rows(key)
    scales = column_scale(key)
    vectors = picked_rows(key, basis, 500) + 0.5 * picked_rows(key, basis, 600)
    vectors = vectors + 0.8 * noise_part(key, PANELS - 1, scales) + 0.5 * noise_part(key, 0, scales)
    vectors = vectors + 0.7 * noise_part(key, 50, scales)
    return vectors.astype(jnp.bfloat16)


def setup_inputs(seed: int = 0) -> dict:
    key_list = jax.random.split(jax.random.key(seed), 4)
    earlier = draw_earlier(jax.random.fold_in(key_list[3], 71), 0)
    panels = draw_panels(jax.random.fold_in(key_list[3], 71), 0)
    further = draw_further(jax.random.fold_in(key_list[3], 71), 0)
    return {"earlier": earlier, "panels": panels, "further": further}


def factor_inverse(gram_matrix):
    lower_factor = jnp.linalg.cholesky(gram_matrix)
    identity = jnp.broadcast_to(jnp.eye(gram_matrix.shape[-1], dtype=gram_matrix.dtype), gram_matrix.shape)
    return lax.linalg.triangular_solve(lower_factor, identity, left_side=True, lower=True)

def one_block(earlier, panels, further):
    basis = earlier
    finished = []
    for panel_index in range(PANELS):
        vectors = panels[panel_index]
        coeffs = (jnp.dot(basis.astype(jnp.float32), vectors.T.astype(jnp.float32), preferred_element_type=jnp.float32) / BLEN).astype(jnp.bfloat16)
        removed = jnp.dot(coeffs.T.astype(jnp.float32), basis.astype(jnp.float32), preferred_element_type=jnp.float32)
        residual = (vectors.astype(jnp.float32) - removed).astype(jnp.bfloat16)
        gram_matrix = jnp.dot(residual.astype(jnp.float32), residual.T.astype(jnp.float32), preferred_element_type=jnp.float32) / BLEN
        inverse = factor_inverse(gram_matrix)
        residual_wide = lax.optimization_barrier(residual).astype(jnp.float32)
        fresh = jnp.dot(inverse, residual_wide, precision=lax.Precision.HIGHEST).astype(jnp.bfloat16)
        finished.append(fresh)
        basis = jnp.concatenate([basis, fresh], axis=0)
    coarse = jnp.dot(further.astype(jnp.float32), basis.T.astype(jnp.float32), preferred_element_type=jnp.float32) / BLEN
    return (jnp.stack(finished, 0), coarse)

def reference(earlier, panels, further):

    def per_block(block_index):
        return one_block(lax.dynamic_index_in_dim(earlier, block_index, 1, keepdims=False), lax.dynamic_index_in_dim(panels, block_index, 2, keepdims=False), lax.dynamic_index_in_dim(further, block_index, 1, keepdims=False))
    new_stack, coarse_stack = lax.map(per_block, jnp.arange(NBLK, dtype=jnp.int32))
    return (jnp.transpose(new_stack, (1, 2, 0, 3)), jnp.transpose(coarse_stack, (1, 0, 2)))
```

```python
import jax
import jax.numpy as jnp
from jax import lax
from jax.sharding import PartitionSpec as P


def factor_inverse(gram_matrix):
    lower_factor = jnp.linalg.cholesky(gram_matrix)
    identity = jnp.broadcast_to(
        jnp.eye(gram_matrix.shape[-1], dtype=gram_matrix.dtype), gram_matrix.shape
    )
    return lax.linalg.triangular_solve(lower_factor, identity, left_side=True, lower=True)


def send(arriving):
    return lax.all_to_all(
        arriving[None], ("lat", "mode"), split_axis=2, concat_axis=0, tiled=True
    )


def arrange(received):
    lat_count = lax.axis_size("lat")
    mode_count = lax.axis_size("mode")
    vector_part = received.shape[1]
    block_count = received.shape[2]
    entry_part = received.shape[3]
    received = received.reshape(lat_count, mode_count, vector_part, block_count, entry_part)
    received = received.transpose(1, 2, 3, 0, 4)
    return received.reshape(mode_count * vector_part, block_count, lat_count * entry_part)


def project(earlier, finished, vectors, block_len):
    pieces = [earlier] + finished
    removed = None
    for basis_part in pieces:
        coeffs = (
            jnp.einsum("nbl,pbl->bnp", basis_part, vectors, preferred_element_type=jnp.float32)
            / block_len
        )
        coeffs = coeffs.astype(jnp.bfloat16)
        term = jnp.einsum("bnp,nbl->pbl", coeffs, basis_part, preferred_element_type=jnp.float32)
        removed = term if removed is None else removed + term
    residual = (vectors.astype(jnp.float32) - removed).astype(jnp.bfloat16)
    gram_matrix = (
        jnp.einsum("pbl,qbl->bpq", residual, residual, preferred_element_type=jnp.float32)
        / block_len
    )
    inverse = factor_inverse(gram_matrix)
    residual_wide = lax.optimization_barrier(residual).astype(jnp.float32)
    fresh = jnp.einsum("bpq,qbl->pbl", inverse, residual_wide, precision=lax.Precision.HIGHEST)
    return fresh.astype(jnp.bfloat16)


def per_device(earlier, panels, further):
    block_len = earlier.shape[2]
    panel_count = panels.shape[0]
    arrived = [send(panels[0])]
    for panel_index in range(1, panel_count):
        outgoing, arrived[-1] = lax.optimization_barrier((panels[panel_index], arrived[-1]))
        arrived.append(send(outgoing))
    outgoing, arrived[-1] = lax.optimization_barrier((further, arrived[-1]))
    further_arrived = send(outgoing)
    finished = []
    for panel_index in range(panel_count):
        vectors = arrange(arrived[panel_index])
        finished.append(project(earlier, finished, vectors, block_len))
    finished, further_arrived = lax.optimization_barrier((finished, further_arrived))
    further_blocks = arrange(further_arrived)
    products = []
    for basis_part in [earlier] + finished:
        products.append(
            jnp.einsum(
                "nbl,pbl->pbn", basis_part, further_blocks, preferred_element_type=jnp.float32
            )
            / block_len
        )
    coarse = jnp.concatenate(products, axis=2)
    return (jnp.stack(finished, 0), coarse)


def solution(mesh):
    return jax.shard_map(
        per_device,
        mesh=mesh,
        in_specs=(
            P(None, ("lat", "mode"), None),
            P(None, "mode", None, "lat"),
            P("mode", None, "lat"),
        ),
        out_specs=(P(None, None, ("lat", "mode"), None), P(None, ("lat", "mode"), None)),
        check_vma=False,
    )
```

```python
import jax
import jax.numpy as jnp
from jax import lax
from jax.sharding import PartitionSpec as P


def factor_inverse(gram_matrix):
    lower_factor = jnp.linalg.cholesky(gram_matrix)
    identity = jnp.broadcast_to(
        jnp.eye(gram_matrix.shape[-1], dtype=gram_matrix.dtype), gram_matrix.shape
    )
    return lax.linalg.triangular_solve(lower_factor, identity, left_side=True, lower=True)


def send(block_major):
    return lax.all_to_all(block_major, ("lat", "mode"), split_axis=0, concat_axis=0, tiled=True)


def split_by_source(received):
    lat_count = lax.axis_size("lat")
    mode_count = lax.axis_size("mode")
    return received.reshape(lat_count, mode_count, received.shape[1], received.shape[2])


def arrange(received):
    by_source = split_by_source(received)
    lat_count, mode_count, vector_part, entry_part = by_source.shape
    whole = by_source.transpose(1, 2, 0, 3)
    return whole.reshape(mode_count * vector_part, 1, lat_count * entry_part)


def project(earlier, finished, vectors, block_len):
    pieces = [earlier] + finished
    removed = None
    for basis_part in pieces:
        coeffs = (
            jnp.einsum("nbl,pbl->bnp", basis_part, vectors, preferred_element_type=jnp.float32)
            / block_len
        )
        coeffs = coeffs.astype(jnp.bfloat16)
        term = jnp.einsum("bnp,nbl->pbl", coeffs, basis_part, preferred_element_type=jnp.float32)
        removed = term if removed is None else removed + term
    residual = (vectors.astype(jnp.float32) - removed).astype(jnp.bfloat16)
    gram_matrix = (
        jnp.einsum("pbl,qbl->bpq", residual, residual, preferred_element_type=jnp.float32)
        / block_len
    )
    inverse = factor_inverse(gram_matrix)
    residual_wide = lax.optimization_barrier(residual).astype(jnp.float32)
    fresh = jnp.einsum("bpq,qbl->pbl", inverse, residual_wide, precision=lax.Precision.HIGHEST)
    return fresh.astype(jnp.bfloat16)


def per_device(earlier, panels, further):
    block_len = earlier.shape[2]
    panel_count = panels.shape[0]
    outgoing = [panels[k].transpose(1, 0, 2) for k in range(panel_count)]
    outgoing.append(further.transpose(1, 0, 2))
    arrived = [send(outgoing[0])]
    for index in range(1, len(outgoing)):
        ready, arrived[-1] = lax.optimization_barrier((outgoing[index], arrived[-1]))
        arrived.append(send(ready))
    finished = []
    for panel_index in range(panel_count):
        vectors = arrange(arrived[panel_index])
        finished.append(project(earlier, finished, vectors, block_len))
    finished, further_arrived = lax.optimization_barrier((finished, arrived[-1]))
    new_basis = jnp.stack(finished, 0)
    further_blocks = arrange(further_arrived)
    products = []
    for basis_part in [earlier] + finished:
        products.append(
            jnp.einsum(
                "nbl,pbl->pbn", basis_part, further_blocks, preferred_element_type=jnp.float32
            )
            / block_len
        )
    coarse = jnp.concatenate(products, axis=2)
    return (new_basis, coarse)


def solution(mesh):
    return jax.shard_map(
        per_device,
        mesh=mesh,
        in_specs=(
            P(None, ("lat", "mode"), None),
            P(None, "mode", None, "lat"),
            P("mode", None, "lat"),
        ),
        out_specs=(P(None, None, ("lat", "mode"), None), P(None, ("lat", "mode"), None)),
        check_vma=False,
    )
```

```python
import functools

import jax
import jax.numpy as jnp
from jax import lax
from jax.experimental import pallas as pl
from jax.experimental.pallas import tpu as pltpu
from jax.sharding import PartitionSpec as P

NT = (((1,), (1,)), ((), ()))


def project_kernel(*refs, piece_count, block_len):
    basis_refs = refs[:piece_count]
    vectors_ref, residual_ref, gram_ref = refs[piece_count:]
    vectors = vectors_ref[...]
    removed = None
    for basis_ref in basis_refs:
        basis = basis_ref[...]
        coeffs_t = lax.dot_general(vectors, basis, NT, preferred_element_type=jnp.float32)
        coeffs_t = (coeffs_t / block_len).astype(jnp.bfloat16)
        term = jnp.dot(coeffs_t, basis, preferred_element_type=jnp.float32)
        removed = term if removed is None else removed + term
    residual = (vectors.astype(jnp.float32) - removed).astype(jnp.bfloat16)
    residual_ref[...] = residual
    gram_ref[...] = lax.dot_general(residual, residual, NT, preferred_element_type=jnp.float32) / block_len


def project_call(pieces, vectors):
    count, block_len = vectors.shape
    rows = sum(p.shape[0] for p in pieces)
    spec = pl.BlockSpec(memory_space=pltpu.MemorySpace.VMEM)
    return pl.pallas_call(
        functools.partial(project_kernel, piece_count=len(pieces), block_len=block_len),
        out_shape=(
            jax.ShapeDtypeStruct((count, block_len), jnp.bfloat16),
            jax.ShapeDtypeStruct((count, count), jnp.float32),
        ),
        in_specs=[spec] * (len(pieces) + 1),
        out_specs=(spec, spec),
        compiler_params=pltpu.CompilerParams(vmem_limit_bytes=48 * 1024 * 1024),
        cost_estimate=pl.CostEstimate(
            flops=4 * rows * count * block_len + 2 * count * count * block_len,
            transcendentals=0,
            bytes_accessed=2 * block_len * (rows + 2 * count) + 4 * count * count,
        ),
    )(*pieces, vectors)


def factor_inverse(gram_matrix):
    lower_factor = jnp.linalg.cholesky(gram_matrix)
    identity = jnp.broadcast_to(
        jnp.eye(gram_matrix.shape[-1], dtype=gram_matrix.dtype), gram_matrix.shape
    )
    return lax.linalg.triangular_solve(lower_factor, identity, left_side=True, lower=True)


def send(block_major):
    return lax.all_to_all(block_major, ("lat", "mode"), split_axis=0, concat_axis=0, tiled=True)


def split_by_source(received):
    lat_count = lax.axis_size("lat")
    mode_count = lax.axis_size("mode")
    return received.reshape(lat_count, mode_count, received.shape[1], received.shape[2])


def arrange(received):
    by_source = split_by_source(received)
    lat_count, mode_count, vector_part, entry_part = by_source.shape
    whole = by_source.transpose(1, 2, 0, 3)
    return whole.reshape(mode_count * vector_part, 1, lat_count * entry_part)


def project(earlier, finished, vectors, block_len):
    count = vectors.shape[0]
    pieces = [piece.reshape(piece.shape[0], block_len) for piece in [earlier] + finished]
    residual, gram_matrix = project_call(pieces, vectors.reshape(count, block_len))
    inverse = factor_inverse(gram_matrix)
    fresh = jnp.dot(inverse, residual.astype(jnp.float32), precision=lax.Precision.HIGHEST)
    return fresh.astype(jnp.bfloat16).reshape(count, 1, block_len)


def per_device(earlier, panels, further):
    block_len = earlier.shape[2]
    panel_count = panels.shape[0]
    outgoing = [panels[k].transpose(1, 0, 2) for k in range(panel_count)]
    outgoing.append(further.transpose(1, 0, 2))
    arrived = [send(outgoing[0])]
    for index in range(1, len(outgoing)):
        ready, arrived[-1] = lax.optimization_barrier((outgoing[index], arrived[-1]))
        arrived.append(send(ready))
    finished = []
    for panel_index in range(panel_count):
        vectors = arrange(arrived[panel_index])
        finished.append(project(earlier, finished, vectors, block_len))
    finished, further_arrived = lax.optimization_barrier((finished, arrived[-1]))
    new_basis = jnp.stack(finished, 0)
    further_blocks = arrange(further_arrived)
    products = []
    for basis_part in [earlier] + finished:
        products.append(
            jnp.einsum(
                "nbl,pbl->pbn", basis_part, further_blocks, preferred_element_type=jnp.float32
            )
            / block_len
        )
    coarse = jnp.concatenate(products, axis=2)
    return (new_basis, coarse)


def solution(mesh):
    return jax.shard_map(
        per_device,
        mesh=mesh,
        in_specs=(
            P(None, ("lat", "mode"), None),
            P(None, "mode", None, "lat"),
            P("mode", None, "lat"),
        ),
        out_specs=(P(None, None, ("lat", "mode"), None), P(None, ("lat", "mode"), None)),
        check_vma=False,
    )
```

```python
import functools

import jax
import jax.numpy as jnp
from jax import lax
from jax.experimental import pallas as pl
from jax.experimental.pallas import tpu as pltpu
from jax.sharding import PartitionSpec as P

NT = (((1,), (1,)), ((), ()))


def project_kernel(*refs, piece_count, block_len):
    basis_refs = refs[:piece_count]
    vectors_ref, residual_ref, gram_ref = refs[piece_count:]
    vectors = vectors_ref[...]
    removed = None
    for basis_ref in basis_refs:
        basis = basis_ref[...]
        coeffs_t = lax.dot_general(vectors, basis, NT, preferred_element_type=jnp.float32)
        coeffs_t = (coeffs_t / block_len).astype(jnp.bfloat16)
        term = jnp.dot(coeffs_t, basis, preferred_element_type=jnp.float32)
        removed = term if removed is None else removed + term
    residual = (vectors.astype(jnp.float32) - removed).astype(jnp.bfloat16)
    residual_ref[...] = residual
    gram_ref[...] = lax.dot_general(residual, residual, NT, preferred_element_type=jnp.float32) / block_len


def project_call(pieces, vectors):
    count, block_len = vectors.shape
    rows = sum(p.shape[0] for p in pieces)
    spec = pl.BlockSpec(memory_space=pltpu.MemorySpace.VMEM)
    return pl.pallas_call(
        functools.partial(project_kernel, piece_count=len(pieces), block_len=block_len),
        out_shape=(
            jax.ShapeDtypeStruct((count, block_len), jnp.bfloat16),
            jax.ShapeDtypeStruct((count, count), jnp.float32),
        ),
        in_specs=[spec] * (len(pieces) + 1),
        out_specs=(spec, spec),
        compiler_params=pltpu.CompilerParams(vmem_limit_bytes=48 * 1024 * 1024),
        cost_estimate=pl.CostEstimate(
            flops=4 * rows * count * block_len + 2 * count * count * block_len,
            transcendentals=0,
            bytes_accessed=2 * block_len * (rows + 2 * count) + 4 * count * count,
        ),
    )(*pieces, vectors)


def coarse_kernel(*refs, piece_count):
    further_ref = refs[0]
    basis_refs = refs[1:1 + piece_count]
    out_refs = refs[1 + piece_count:]
    for mode_index in range(further_ref.shape[1]):
        vectors = further_ref[0, mode_index]
        for basis_ref, out_ref in zip(basis_refs, out_refs):
            out_ref[0, mode_index] = lax.dot_general(
                vectors, basis_ref[...], NT, preferred_element_type=jnp.float32
            )


def coarse_call(further_parts, pieces):
    lat_count, mode_count, vector_part, entry_part = further_parts.shape
    rows = sum(p.shape[0] for p in pieces)
    further_spec = pl.BlockSpec((1, mode_count, vector_part, entry_part), lambda l: (l, 0, 0, 0))
    piece_specs = [pl.BlockSpec((p.shape[0], entry_part), lambda l: (0, l)) for p in pieces]
    out_specs = [
        pl.BlockSpec((1, mode_count, vector_part, p.shape[0]), lambda l: (l, 0, 0, 0)) for p in pieces
    ]
    out_shape = [
        jax.ShapeDtypeStruct((lat_count, mode_count, vector_part, p.shape[0]), jnp.float32)
        for p in pieces
    ]
    block_len = lat_count * entry_part
    return pl.pallas_call(
        functools.partial(coarse_kernel, piece_count=len(pieces)),
        grid=(lat_count,),
        out_shape=out_shape,
        in_specs=[further_spec] + piece_specs,
        out_specs=out_specs,
        cost_estimate=pl.CostEstimate(
            flops=2 * rows * mode_count * vector_part * block_len,
            transcendentals=0,
            bytes_accessed=2 * block_len * (rows + mode_count * vector_part),
        ),
    )(further_parts, *pieces)


def factor_inverse(gram_matrix):
    lower_factor = jnp.linalg.cholesky(gram_matrix)
    identity = jnp.broadcast_to(
        jnp.eye(gram_matrix.shape[-1], dtype=gram_matrix.dtype), gram_matrix.shape
    )
    return lax.linalg.triangular_solve(lower_factor, identity, left_side=True, lower=True)


def send(block_major):
    return lax.all_to_all(block_major, ("lat", "mode"), split_axis=0, concat_axis=0, tiled=True)


def split_by_source(received):
    lat_count = lax.axis_size("lat")
    mode_count = lax.axis_size("mode")
    return received.reshape(lat_count, mode_count, received.shape[1], received.shape[2])


def arrange(received):
    by_source = split_by_source(received)
    lat_count, mode_count, vector_part, entry_part = by_source.shape
    whole = by_source.transpose(1, 2, 0, 3)
    return whole.reshape(mode_count * vector_part, 1, lat_count * entry_part)


def project(earlier, finished, vectors, block_len):
    count = vectors.shape[0]
    pieces = [piece.reshape(piece.shape[0], block_len) for piece in [earlier] + finished]
    residual, gram_matrix = project_call(pieces, vectors.reshape(count, block_len))
    inverse = factor_inverse(gram_matrix)
    fresh = jnp.dot(inverse, residual.astype(jnp.float32), precision=lax.Precision.HIGHEST)
    return fresh.astype(jnp.bfloat16).reshape(count, 1, block_len)


def per_device(earlier, panels, further):
    block_len = earlier.shape[2]
    panel_count = panels.shape[0]
    outgoing = [panels[k].transpose(1, 0, 2) for k in range(panel_count)]
    outgoing.append(further.transpose(1, 0, 2))
    arrived = [send(outgoing[0])]
    for index in range(1, len(outgoing)):
        ready, arrived[-1] = lax.optimization_barrier((outgoing[index], arrived[-1]))
        arrived.append(send(ready))
    finished = []
    for panel_index in range(panel_count):
        vectors = arrange(arrived[panel_index])
        finished.append(project(earlier, finished, vectors, block_len))
    finished, further_arrived = lax.optimization_barrier((finished, arrived[-1]))
    new_basis = jnp.stack(finished, 0)
    further_parts = split_by_source(further_arrived)
    pieces = [piece.reshape(piece.shape[0], block_len) for piece in [earlier] + finished]
    partials = coarse_call(further_parts, pieces)
    count = further_parts.shape[1] * further_parts.shape[2]
    coarse = jnp.concatenate([partial.sum(0) for partial in partials], axis=-1)
    coarse = (coarse / block_len).reshape(count, 1, -1)
    return (new_basis, coarse)


def solution(mesh):
    return jax.shard_map(
        per_device,
        mesh=mesh,
        in_specs=(
            P(None, ("lat", "mode"), None),
            P(None, "mode", None, "lat"),
            P("mode", None, "lat"),
        ),
        out_specs=(P(None, None, ("lat", "mode"), None), P(None, ("lat", "mode"), None)),
        check_vma=False,
    )
```

```python
import functools

import jax
import jax.numpy as jnp
from jax import lax
from jax.experimental import pallas as pl
from jax.experimental.pallas import tpu as pltpu
from jax.sharding import PartitionSpec as P

NT = (((1,), (1,)), ((), ()))


def project_kernel(*refs, piece_count, block_len):
    basis_refs = refs[:piece_count]
    vectors_ref, residual_ref, gram_ref = refs[piece_count:]
    vectors = vectors_ref[...]
    removed = None
    for basis_ref in basis_refs:
        basis = basis_ref[...]
        coeffs_t = lax.dot_general(vectors, basis, NT, preferred_element_type=jnp.float32)
        coeffs_t = (coeffs_t / block_len).astype(jnp.bfloat16)
        term = jnp.dot(coeffs_t, basis, preferred_element_type=jnp.float32)
        removed = term if removed is None else removed + term
    residual = (vectors.astype(jnp.float32) - removed).astype(jnp.bfloat16)
    residual_ref[...] = residual
    gram_ref[...] = lax.dot_general(residual, residual, NT, preferred_element_type=jnp.float32) / block_len


def project_call(pieces, vectors):
    count, block_len = vectors.shape
    rows = sum(p.shape[0] for p in pieces)
    spec = pl.BlockSpec(memory_space=pltpu.MemorySpace.VMEM)
    return pl.pallas_call(
        functools.partial(project_kernel, piece_count=len(pieces), block_len=block_len),
        out_shape=(
            jax.ShapeDtypeStruct((count, block_len), jnp.bfloat16),
            jax.ShapeDtypeStruct((count, count), jnp.float32),
        ),
        in_specs=[spec] * (len(pieces) + 1),
        out_specs=(spec, spec),
        compiler_params=pltpu.CompilerParams(vmem_limit_bytes=48 * 1024 * 1024),
        cost_estimate=pl.CostEstimate(
            flops=4 * rows * count * block_len + 2 * count * count * block_len,
            transcendentals=0,
            bytes_accessed=2 * block_len * (rows + 2 * count) + 4 * count * count,
        ),
    )(*pieces, vectors)


def factor_inverse(gram_matrix):
    lower_factor = jnp.linalg.cholesky(gram_matrix)
    identity = jnp.broadcast_to(
        jnp.eye(gram_matrix.shape[-1], dtype=gram_matrix.dtype), gram_matrix.shape
    )
    return lax.linalg.triangular_solve(lower_factor, identity, left_side=True, lower=True)


def send(block_major):
    return lax.all_to_all(block_major, ("lat", "mode"), split_axis=0, concat_axis=0, tiled=True)


def split_by_source(received):
    lat_count = lax.axis_size("lat")
    mode_count = lax.axis_size("mode")
    return received.reshape(lat_count, mode_count, received.shape[1], received.shape[2])


def arrange(received):
    by_source = split_by_source(received)
    lat_count, mode_count, vector_part, entry_part = by_source.shape
    whole = by_source.transpose(1, 2, 0, 3)
    return whole.reshape(mode_count * vector_part, 1, lat_count * entry_part)


def project(earlier, finished, vectors, block_len):
    count = vectors.shape[0]
    pieces = [piece.reshape(piece.shape[0], block_len) for piece in [earlier] + finished]
    residual, gram_matrix = project_call(pieces, vectors.reshape(count, block_len))
    inverse = factor_inverse(gram_matrix)
    fresh = jnp.dot(inverse, residual.astype(jnp.float32), precision=lax.Precision.HIGHEST)
    return fresh.astype(jnp.bfloat16).reshape(count, 1, block_len)


def per_device(earlier, panels, further):
    block_len = earlier.shape[2]
    panel_count = panels.shape[0]
    outgoing = [panels[k].transpose(1, 0, 2) for k in range(panel_count)]
    outgoing.append(further.transpose(1, 0, 2))
    arrived = [send(outgoing[0])]
    for index in range(1, len(outgoing)):
        ready, arrived[0] = lax.optimization_barrier((outgoing[index], arrived[0]))
        arrived.append(send(ready))
    finished = []
    for panel_index in range(panel_count):
        vectors = arrange(arrived[panel_index])
        finished.append(project(earlier, finished, vectors, block_len))
    new_basis = jnp.stack(finished, 0)
    finished, further_arrived = lax.optimization_barrier((finished, arrived[-1]))
    further_blocks = arrange(further_arrived)
    products = []
    for basis_part in [earlier] + finished:
        products.append(
            jnp.einsum(
                "nbl,pbl->pbn", basis_part, further_blocks, preferred_element_type=jnp.float32
            )
            / block_len
        )
    coarse = jnp.concatenate(products, axis=2)
    return (new_basis, coarse)


def solution(mesh):
    return jax.shard_map(
        per_device,
        mesh=mesh,
        in_specs=(
            P(None, ("lat", "mode"), None),
            P(None, "mode", None, "lat"),
            P("mode", None, "lat"),
        ),
        out_specs=(P(None, None, ("lat", "mode"), None), P(None, ("lat", "mode"), None)),
        check_vma=False,
    )
```

```python
import functools

import jax
import jax.numpy as jnp
from jax import lax
from jax.experimental import pallas as pl
from jax.experimental.pallas import tpu as pltpu
from jax.sharding import PartitionSpec as P

NT = (((1,), (1,)), ((), ()))


def project_kernel(*refs, piece_count, block_len):
    basis_refs = refs[:piece_count]
    vectors_ref, residual_ref, gram_ref = refs[piece_count:]
    vectors = vectors_ref[...]
    removed = None
    for basis_ref in basis_refs:
        basis = basis_ref[...]
        coeffs_t = lax.dot_general(vectors, basis, NT, preferred_element_type=jnp.float32)
        coeffs_t = (coeffs_t / block_len).astype(jnp.bfloat16)
        term = jnp.dot(coeffs_t, basis, preferred_element_type=jnp.float32)
        removed = term if removed is None else removed + term
    residual = (vectors.astype(jnp.float32) - removed).astype(jnp.bfloat16)
    residual_ref[...] = residual
    gram_ref[...] = lax.dot_general(residual, residual, NT, preferred_element_type=jnp.float32) / block_len


def project_call(pieces, vectors):
    count, block_len = vectors.shape
    rows = sum(p.shape[0] for p in pieces)
    spec = pl.BlockSpec(memory_space=pltpu.MemorySpace.VMEM)
    return pl.pallas_call(
        functools.partial(project_kernel, piece_count=len(pieces), block_len=block_len),
        out_shape=(
            jax.ShapeDtypeStruct((count, block_len), jnp.bfloat16),
            jax.ShapeDtypeStruct((count, count), jnp.float32),
        ),
        in_specs=[spec] * (len(pieces) + 1),
        out_specs=(spec, spec),
        compiler_params=pltpu.CompilerParams(vmem_limit_bytes=48 * 1024 * 1024),
        cost_estimate=pl.CostEstimate(
            flops=4 * rows * count * block_len + 2 * count * count * block_len,
            transcendentals=0,
            bytes_accessed=2 * block_len * (rows + 2 * count) + 4 * count * count,
        ),
    )(*pieces, vectors)


def factor_inverse(gram_matrix):
    lower_factor = jnp.linalg.cholesky(gram_matrix)
    identity = jnp.broadcast_to(
        jnp.eye(gram_matrix.shape[-1], dtype=gram_matrix.dtype), gram_matrix.shape
    )
    return lax.linalg.triangular_solve(lower_factor, identity, left_side=True, lower=True)


def send(block_major):
    return lax.all_to_all(block_major, ("lat", "mode"), split_axis=0, concat_axis=0, tiled=True)


def split_by_source(received):
    lat_count = lax.axis_size("lat")
    mode_count = lax.axis_size("mode")
    return received.reshape(lat_count, mode_count, received.shape[1], received.shape[2])


def arrange(received):
    by_source = split_by_source(received)
    lat_count, mode_count, vector_part, entry_part = by_source.shape
    whole = by_source.transpose(1, 2, 0, 3)
    return whole.reshape(mode_count * vector_part, 1, lat_count * entry_part)


def project(earlier, finished, vectors, block_len):
    count = vectors.shape[0]
    pieces = [piece.reshape(piece.shape[0], block_len) for piece in [earlier] + finished]
    residual, gram_matrix = project_call(pieces, vectors.reshape(count, block_len))
    inverse = factor_inverse(gram_matrix)
    fresh = jnp.dot(inverse, residual.astype(jnp.float32), precision=lax.Precision.HIGHEST)
    return fresh.astype(jnp.bfloat16).reshape(count, 1, block_len)


def per_device(earlier, panels, further):
    block_len = earlier.shape[2]
    panel_count = panels.shape[0]
    outgoing = [panels[k].transpose(1, 0, 2) for k in range(panel_count)]
    outgoing.append(further.transpose(1, 0, 2))
    arrived = [send(outgoing[0])]
    for index in range(1, len(outgoing)):
        ready, arrived[0] = lax.optimization_barrier((outgoing[index], arrived[0]))
        arrived.append(send(ready))
    finished = []
    for panel_index in range(panel_count):
        vectors = arrange(arrived[panel_index])
        finished.append(project(earlier, finished, vectors, block_len))
    new_basis = jnp.stack(finished, 0)
    new_basis, finished, further_arrived = lax.optimization_barrier((new_basis, finished, arrived[-1]))
    further_blocks = arrange(further_arrived)
    products = []
    for basis_part in [earlier] + finished:
        products.append(
            jnp.einsum(
                "nbl,pbl->pbn", basis_part, further_blocks, preferred_element_type=jnp.float32
            )
            / block_len
        )
    coarse = jnp.concatenate(products, axis=2)
    return (new_basis, coarse)


def solution(mesh):
    return jax.shard_map(
        per_device,
        mesh=mesh,
        in_specs=(
            P(None, ("lat", "mode"), None),
            P(None, "mode", None, "lat"),
            P("mode", None, "lat"),
        ),
        out_specs=(P(None, None, ("lat", "mode"), None), P(None, ("lat", "mode"), None)),
        check_vma=False,
    )
```

```python
import functools

import jax
import jax.numpy as jnp
from jax import lax
from jax.experimental import pallas as pl
from jax.experimental.pallas import tpu as pltpu
from jax.sharding import PartitionSpec as P

NT = (((1,), (1,)), ((), ()))


def project_kernel(*refs, piece_count, block_len):
    basis_refs = refs[:piece_count]
    vectors_ref, residual_ref, gram_ref = refs[piece_count:]
    vectors = vectors_ref[...]
    removed = None
    for basis_ref in basis_refs:
        basis = basis_ref[...]
        coeffs_t = lax.dot_general(vectors, basis, NT, preferred_element_type=jnp.float32)
        coeffs_t = (coeffs_t / block_len).astype(jnp.bfloat16)
        term = jnp.dot(coeffs_t, basis, preferred_element_type=jnp.float32)
        removed = term if removed is None else removed + term
    residual = (vectors.astype(jnp.float32) - removed).astype(jnp.bfloat16)
    residual_ref[...] = residual
    gram_ref[...] = lax.dot_general(residual, residual, NT, preferred_element_type=jnp.float32) / block_len


def project_call(pieces, vectors):
    count, block_len = vectors.shape
    rows = sum(p.shape[0] for p in pieces)
    spec = pl.BlockSpec(memory_space=pltpu.MemorySpace.VMEM)
    return pl.pallas_call(
        functools.partial(project_kernel, piece_count=len(pieces), block_len=block_len),
        out_shape=(
            jax.ShapeDtypeStruct((count, block_len), jnp.bfloat16),
            jax.ShapeDtypeStruct((count, count), jnp.float32),
        ),
        in_specs=[spec] * (len(pieces) + 1),
        out_specs=(spec, spec),
        compiler_params=pltpu.CompilerParams(vmem_limit_bytes=48 * 1024 * 1024),
        cost_estimate=pl.CostEstimate(
            flops=4 * rows * count * block_len + 2 * count * count * block_len,
            transcendentals=0,
            bytes_accessed=2 * block_len * (rows + 2 * count) + 4 * count * count,
        ),
    )(*pieces, vectors)


def factor_inverse(gram_matrix):
    lower_factor = jnp.linalg.cholesky(gram_matrix)
    identity = jnp.broadcast_to(
        jnp.eye(gram_matrix.shape[-1], dtype=gram_matrix.dtype), gram_matrix.shape
    )
    return lax.linalg.triangular_solve(lower_factor, identity, left_side=True, lower=True)


def send(block_major):
    return lax.all_to_all(block_major, ("lat", "mode"), split_axis=0, concat_axis=0, tiled=True)


def split_by_source(received):
    lat_count = lax.axis_size("lat")
    mode_count = lax.axis_size("mode")
    return received.reshape(lat_count, mode_count, received.shape[1], received.shape[2])


def arrange(received):
    by_source = split_by_source(received)
    lat_count, mode_count, vector_part, entry_part = by_source.shape
    whole = by_source.transpose(1, 2, 0, 3)
    return whole.reshape(mode_count * vector_part, 1, lat_count * entry_part)


def project(earlier, finished, vectors, block_len):
    count = vectors.shape[0]
    pieces = [piece.reshape(piece.shape[0], block_len) for piece in [earlier] + finished]
    residual, gram_matrix = project_call(pieces, vectors.reshape(count, block_len))
    inverse = factor_inverse(gram_matrix)
    fresh = jnp.dot(inverse, residual.astype(jnp.float32), precision=lax.Precision.HIGHEST)
    return fresh.astype(jnp.bfloat16).reshape(count, 1, block_len)


def per_device(earlier, panels, further):
    block_len = earlier.shape[2]
    panel_count = panels.shape[0]
    outgoing = [panels[k].transpose(1, 0, 2) for k in range(panel_count)]
    outgoing.append(further.transpose(1, 0, 2))
    arrived = [send(outgoing[0])]
    for index in range(1, len(outgoing)):
        ready, arrived[0] = lax.optimization_barrier((outgoing[index], arrived[0]))
        arrived.append(send(ready))
    finished = []
    for panel_index in range(panel_count):
        vectors = arrange(arrived[panel_index])
        finished.append(project(earlier, finished, vectors, block_len))
    new_basis = jnp.stack(finished, 0)
    full_basis = jnp.concatenate([earlier] + finished, axis=0)
    new_basis, full_basis, further_arrived = lax.optimization_barrier(
        (new_basis, full_basis, arrived[-1])
    )
    further_blocks = arrange(further_arrived)
    coarse = (
        jnp.einsum("nbl,pbl->pbn", full_basis, further_blocks, preferred_element_type=jnp.float32)
        / block_len
    )
    return (new_basis, coarse)


def solution(mesh):
    return jax.shard_map(
        per_device,
        mesh=mesh,
        in_specs=(
            P(None, ("lat", "mode"), None),
            P(None, "mode", None, "lat"),
            P("mode", None, "lat"),
        ),
        out_specs=(P(None, None, ("lat", "mode"), None), P(None, ("lat", "mode"), None)),
        check_vma=False,
    )
```

```python
import functools

import jax
import jax.numpy as jnp
from jax import lax
from jax.experimental import pallas as pl
from jax.experimental.pallas import tpu as pltpu
from jax.sharding import PartitionSpec as P

NT = (((1,), (1,)), ((), ()))


def project_kernel(*refs, piece_count, block_len):
    basis_refs = refs[:piece_count]
    vectors_ref, residual_ref, gram_ref = refs[piece_count:]
    vectors = vectors_ref[...]
    removed = None
    for basis_ref in basis_refs:
        basis = basis_ref[...]
        coeffs_t = lax.dot_general(vectors, basis, NT, preferred_element_type=jnp.float32)
        coeffs_t = (coeffs_t / block_len).astype(jnp.bfloat16)
        term = jnp.dot(coeffs_t, basis, preferred_element_type=jnp.float32)
        removed = term if removed is None else removed + term
    residual = (vectors.astype(jnp.float32) - removed).astype(jnp.bfloat16)
    residual_ref[...] = residual
    gram_ref[...] = lax.dot_general(residual, residual, NT, preferred_element_type=jnp.float32) / block_len


def project_call(pieces, vectors):
    count, block_len = vectors.shape
    rows = sum(p.shape[0] for p in pieces)
    spec = pl.BlockSpec(memory_space=pltpu.MemorySpace.VMEM)
    return pl.pallas_call(
        functools.partial(project_kernel, piece_count=len(pieces), block_len=block_len),
        out_shape=(
            jax.ShapeDtypeStruct((count, block_len), jnp.bfloat16),
            jax.ShapeDtypeStruct((count, count), jnp.float32),
        ),
        in_specs=[spec] * (len(pieces) + 1),
        out_specs=(spec, spec),
        compiler_params=pltpu.CompilerParams(vmem_limit_bytes=48 * 1024 * 1024),
        cost_estimate=pl.CostEstimate(
            flops=4 * rows * count * block_len + 2 * count * count * block_len,
            transcendentals=0,
            bytes_accessed=2 * block_len * (rows + 2 * count) + 4 * count * count,
        ),
    )(*pieces, vectors)


def factor_inverse(gram_matrix):
    lower_factor = jnp.linalg.cholesky(gram_matrix)
    identity = jnp.broadcast_to(
        jnp.eye(gram_matrix.shape[-1], dtype=gram_matrix.dtype), gram_matrix.shape
    )
    return lax.linalg.triangular_solve(lower_factor, identity, left_side=True, lower=True)


def send(block_major):
    return lax.all_to_all(block_major, ("lat", "mode"), split_axis=0, concat_axis=0, tiled=True)


def split_by_source(received):
    lat_count = lax.axis_size("lat")
    mode_count = lax.axis_size("mode")
    return received.reshape(lat_count, mode_count, received.shape[1], received.shape[2])


def arrange(received):
    by_source = split_by_source(received)
    lat_count, mode_count, vector_part, entry_part = by_source.shape
    whole = by_source.transpose(1, 2, 0, 3)
    return whole.reshape(mode_count * vector_part, 1, lat_count * entry_part)


def project(earlier, finished, vectors, block_len):
    count = vectors.shape[0]
    pieces = [piece.reshape(piece.shape[0], block_len) for piece in [earlier] + finished]
    residual, gram_matrix = project_call(pieces, vectors.reshape(count, block_len))
    inverse = factor_inverse(gram_matrix)
    fresh = jnp.dot(inverse, residual.astype(jnp.float32), precision=lax.Precision.HIGHEST)
    return fresh.astype(jnp.bfloat16).reshape(count, 1, block_len)


def per_device(earlier, panels, further):
    block_len = earlier.shape[2]
    panel_count = panels.shape[0]
    vector_part = panels.shape[1]
    outgoing = panels.transpose(2, 0, 1, 3).reshape(panels.shape[2], -1, panels.shape[3])
    panels_arrived = send(outgoing)
    further_arrived = send(further.transpose(1, 0, 2))
    finished = []
    for panel_index in range(panel_count):
        part = panels_arrived[:, panel_index * vector_part:(panel_index + 1) * vector_part]
        finished.append(project(earlier, finished, arrange(part), block_len))
    new_basis = jnp.stack(finished, 0)
    new_basis, finished, further_arrived = lax.optimization_barrier(
        (new_basis, finished, further_arrived)
    )
    further_blocks = arrange(further_arrived)
    products = []
    for basis_part in [earlier] + finished:
        products.append(
            jnp.einsum(
                "nbl,pbl->pbn", basis_part, further_blocks, preferred_element_type=jnp.float32
            )
            / block_len
        )
    coarse = jnp.concatenate(products, axis=2)
    return (new_basis, coarse)


def solution(mesh):
    return jax.shard_map(
        per_device,
        mesh=mesh,
        in_specs=(
            P(None, ("lat", "mode"), None),
            P(None, "mode", None, "lat"),
            P("mode", None, "lat"),
        ),
        out_specs=(P(None, None, ("lat", "mode"), None), P(None, ("lat", "mode"), None)),
        check_vma=False,
    )
```

```python
import functools

import jax
import jax.numpy as jnp
from jax import lax
from jax.experimental import pallas as pl
from jax.experimental.pallas import tpu as pltpu
from jax.sharding import PartitionSpec as P

NT = (((1,), (1,)), ((), ()))


def project_kernel(*refs, piece_count, block_len):
    basis_refs = refs[:piece_count]
    vectors_ref, residual_ref, gram_ref = refs[piece_count:]
    vectors = vectors_ref[...]
    removed = None
    for basis_ref in basis_refs:
        basis = basis_ref[...]
        coeffs_t = lax.dot_general(vectors, basis, NT, preferred_element_type=jnp.float32)
        coeffs_t = (coeffs_t / block_len).astype(jnp.bfloat16)
        term = jnp.dot(coeffs_t, basis, preferred_element_type=jnp.float32)
        removed = term if removed is None else removed + term
    residual = (vectors.astype(jnp.float32) - removed).astype(jnp.bfloat16)
    residual_ref[...] = residual
    gram_ref[...] = lax.dot_general(residual, residual, NT, preferred_element_type=jnp.float32) / block_len


def project_call(pieces, vectors):
    count, block_len = vectors.shape
    rows = sum(p.shape[0] for p in pieces)
    spec = pl.BlockSpec(memory_space=pltpu.MemorySpace.VMEM)
    return pl.pallas_call(
        functools.partial(project_kernel, piece_count=len(pieces), block_len=block_len),
        out_shape=(
            jax.ShapeDtypeStruct((count, block_len), jnp.bfloat16),
            jax.ShapeDtypeStruct((count, count), jnp.float32),
        ),
        in_specs=[spec] * (len(pieces) + 1),
        out_specs=(spec, spec),
        compiler_params=pltpu.CompilerParams(vmem_limit_bytes=48 * 1024 * 1024),
        cost_estimate=pl.CostEstimate(
            flops=4 * rows * count * block_len + 2 * count * count * block_len,
            transcendentals=0,
            bytes_accessed=2 * block_len * (rows + 2 * count) + 4 * count * count,
        ),
    )(*pieces, vectors)


def factor_inverse(gram_matrix):
    lower_factor = jnp.linalg.cholesky(gram_matrix)
    identity = jnp.broadcast_to(
        jnp.eye(gram_matrix.shape[-1], dtype=gram_matrix.dtype), gram_matrix.shape
    )
    return lax.linalg.triangular_solve(lower_factor, identity, left_side=True, lower=True)


def send(block_major):
    return lax.all_to_all(block_major, ("lat", "mode"), split_axis=0, concat_axis=0, tiled=True)


def split_by_source(received):
    lat_count = lax.axis_size("lat")
    mode_count = lax.axis_size("mode")
    return received.reshape(lat_count, mode_count, received.shape[1], received.shape[2])


def arrange(received):
    by_source = split_by_source(received)
    lat_count, mode_count, vector_part, entry_part = by_source.shape
    whole = by_source.transpose(1, 2, 0, 3)
    return whole.reshape(mode_count * vector_part, 1, lat_count * entry_part)


def project(earlier, finished, vectors, block_len):
    count = vectors.shape[0]
    pieces = [piece.reshape(piece.shape[0], block_len) for piece in [earlier] + finished]
    residual, gram_matrix = project_call(pieces, vectors.reshape(count, block_len))
    inverse = factor_inverse(gram_matrix)
    fresh = jnp.dot(inverse, residual.astype(jnp.float32), precision=lax.Precision.HIGHEST)
    return fresh.astype(jnp.bfloat16).reshape(count, 1, block_len)


def per_device(earlier, panels, further):
    block_len = earlier.shape[2]
    panel_count = panels.shape[0]
    outgoing = panels.transpose(2, 0, 1, 3)
    panels_arrived = send(outgoing)
    further_arrived = send(further.transpose(1, 0, 2))
    finished = []
    for panel_index in range(panel_count):
        part = panels_arrived[:, panel_index]
        finished.append(project(earlier, finished, arrange(part), block_len))
    new_basis = jnp.stack(finished, 0)
    new_basis, finished, further_arrived = lax.optimization_barrier(
        (new_basis, finished, further_arrived)
    )
    further_blocks = arrange(further_arrived)
    products = []
    for basis_part in [earlier] + finished:
        products.append(
            jnp.einsum(
                "nbl,pbl->pbn", basis_part, further_blocks, preferred_element_type=jnp.float32
            )
            / block_len
        )
    coarse = jnp.concatenate(products, axis=2)
    return (new_basis, coarse)


def solution(mesh):
    return jax.shard_map(
        per_device,
        mesh=mesh,
        in_specs=(
            P(None, ("lat", "mode"), None),
            P(None, "mode", None, "lat"),
            P("mode", None, "lat"),
        ),
        out_specs=(P(None, None, ("lat", "mode"), None), P(None, ("lat", "mode"), None)),
        check_vma=False,
    )
```

```python
import functools

import jax
import jax.numpy as jnp
from jax import lax
from jax.experimental import pallas as pl
from jax.experimental.pallas import tpu as pltpu
from jax.sharding import PartitionSpec as P

NT = (((1,), (1,)), ((), ()))


def project_kernel(*refs, piece_count, block_len):
    basis_refs = refs[:piece_count]
    vectors_ref, residual_ref, gram_ref = refs[piece_count:]
    vectors = vectors_ref[...]
    removed = None
    for basis_ref in basis_refs:
        basis = basis_ref[...]
        coeffs_t = lax.dot_general(vectors, basis, NT, preferred_element_type=jnp.float32)
        coeffs_t = (coeffs_t / block_len).astype(jnp.bfloat16)
        term = jnp.dot(coeffs_t, basis, preferred_element_type=jnp.float32)
        removed = term if removed is None else removed + term
    residual = (vectors.astype(jnp.float32) - removed).astype(jnp.bfloat16)
    residual_ref[...] = residual
    gram_ref[...] = lax.dot_general(residual, residual, NT, preferred_element_type=jnp.float32) / block_len


def project_call(pieces, vectors):
    count, block_len = vectors.shape
    rows = sum(p.shape[0] for p in pieces)
    spec = pl.BlockSpec(memory_space=pltpu.MemorySpace.VMEM)
    return pl.pallas_call(
        functools.partial(project_kernel, piece_count=len(pieces), block_len=block_len),
        out_shape=(
            jax.ShapeDtypeStruct((count, block_len), jnp.bfloat16),
            jax.ShapeDtypeStruct((count, count), jnp.float32),
        ),
        in_specs=[spec] * (len(pieces) + 1),
        out_specs=(spec, spec),
        compiler_params=pltpu.CompilerParams(vmem_limit_bytes=48 * 1024 * 1024),
        cost_estimate=pl.CostEstimate(
            flops=4 * rows * count * block_len + 2 * count * count * block_len,
            transcendentals=0,
            bytes_accessed=2 * block_len * (rows + 2 * count) + 4 * count * count,
        ),
    )(*pieces, vectors)


def factor_inverse(gram_matrix):
    lower_factor = jnp.linalg.cholesky(gram_matrix)
    identity = jnp.broadcast_to(
        jnp.eye(gram_matrix.shape[-1], dtype=gram_matrix.dtype), gram_matrix.shape
    )
    return lax.linalg.triangular_solve(lower_factor, identity, left_side=True, lower=True)


def send(block_major):
    return lax.all_to_all(block_major, ("lat", "mode"), split_axis=0, concat_axis=0, tiled=True)


def split_by_source(received):
    lat_count = lax.axis_size("lat")
    mode_count = lax.axis_size("mode")
    return received.reshape(lat_count, mode_count, received.shape[1], received.shape[2])


def arrange(received):
    by_source = split_by_source(received)
    lat_count, mode_count, vector_part, entry_part = by_source.shape
    whole = by_source.transpose(1, 2, 0, 3)
    return whole.reshape(mode_count * vector_part, 1, lat_count * entry_part)


def project(earlier, finished, vectors, block_len):
    count = vectors.shape[0]
    pieces = [piece.reshape(piece.shape[0], block_len) for piece in [earlier] + finished]
    residual, gram_matrix = project_call(pieces, vectors.reshape(count, block_len))
    inverse = factor_inverse(gram_matrix)
    fresh = jnp.dot(inverse, residual.astype(jnp.float32), precision=lax.Precision.HIGHEST)
    return fresh.astype(jnp.bfloat16).reshape(count, 1, block_len)


def per_device(earlier, panels, further):
    block_len = earlier.shape[2]
    panel_count = panels.shape[0]
    vector_part = panels.shape[1]
    outgoing = panels.transpose(2, 0, 1, 3).reshape(panels.shape[2], -1, panels.shape[3])
    panels_arrived = send(outgoing)
    further_arrived = send(further.transpose(1, 0, 2))
    finished = []
    for panel_index in range(panel_count):
        part = panels_arrived[:, panel_index * vector_part:(panel_index + 1) * vector_part]
        finished.append(project(earlier, finished, arrange(part), block_len))
    new_basis = jnp.stack(finished, 0)
    new_basis, finished, further_arrived = lax.optimization_barrier(
        (new_basis, finished, further_arrived)
    )
    lat_count = lax.axis_size("lat")
    further_parts = further_arrived.reshape(lat_count, -1, further_arrived.shape[-1])
    products = []
    for basis_part in [earlier] + finished:
        rows = basis_part.reshape(basis_part.shape[0], lat_count, -1)
        product = jnp.einsum(
            "lpe,jle->lpj", further_parts, rows, preferred_element_type=jnp.float32
        ).sum(0)
        products.append(product.reshape(-1, 1, rows.shape[0]) / block_len)
    coarse = jnp.concatenate(products, axis=2)
    return (new_basis, coarse)


def solution(mesh):
    return jax.shard_map(
        per_device,
        mesh=mesh,
        in_specs=(
            P(None, ("lat", "mode"), None),
            P(None, "mode", None, "lat"),
            P("mode", None, "lat"),
        ),
        out_specs=(P(None, None, ("lat", "mode"), None), P(None, ("lat", "mode"), None)),
        check_vma=False,
    )
```

```python
import functools

import jax
import jax.numpy as jnp
from jax import lax
from jax.experimental import pallas as pl
from jax.experimental.pallas import tpu as pltpu
from jax.sharding import PartitionSpec as P

NT = (((1,), (1,)), ((), ()))


def project_kernel(*refs, piece_count, block_len):
    basis_refs = refs[:piece_count]
    vectors_ref, residual_ref, gram_ref = refs[piece_count:]
    vectors = vectors_ref[...]
    removed = None
    for basis_ref in basis_refs:
        basis = basis_ref[...]
        coeffs_t = lax.dot_general(vectors, basis, NT, preferred_element_type=jnp.float32)
        coeffs_t = (coeffs_t / block_len).astype(jnp.bfloat16)
        term = jnp.dot(coeffs_t, basis, preferred_element_type=jnp.float32)
        removed = term if removed is None else removed + term
    residual = (vectors.astype(jnp.float32) - removed).astype(jnp.bfloat16)
    residual_ref[...] = residual
    gram_ref[...] = lax.dot_general(residual, residual, NT, preferred_element_type=jnp.float32) / block_len


def project_call(pieces, vectors):
    count, block_len = vectors.shape
    rows = sum(p.shape[0] for p in pieces)
    spec = pl.BlockSpec(memory_space=pltpu.MemorySpace.VMEM)
    return pl.pallas_call(
        functools.partial(project_kernel, piece_count=len(pieces), block_len=block_len),
        out_shape=(
            jax.ShapeDtypeStruct((count, block_len), jnp.bfloat16),
            jax.ShapeDtypeStruct((count, count), jnp.float32),
        ),
        in_specs=[spec] * (len(pieces) + 1),
        out_specs=(spec, spec),
        compiler_params=pltpu.CompilerParams(vmem_limit_bytes=48 * 1024 * 1024),
        cost_estimate=pl.CostEstimate(
            flops=4 * rows * count * block_len + 2 * count * count * block_len,
            transcendentals=0,
            bytes_accessed=2 * block_len * (rows + 2 * count) + 4 * count * count,
        ),
    )(*pieces, vectors)


def block_major_kernel(panels_ref, out_ref):
    rows = panels_ref[...]
    rows = rows.reshape(-1, rows.shape[2], rows.shape[3])
    out_ref[...] = jnp.swapaxes(rows, 0, 1)


def block_major(panels, group=16):
    panel_count, vector_part, block_count, entry_part = panels.shape
    group = min(group, block_count)
    return pl.pallas_call(
        block_major_kernel,
        grid=(block_count // group,),
        out_shape=jax.ShapeDtypeStruct(
            (block_count, panel_count * vector_part, entry_part), panels.dtype
        ),
        in_specs=[pl.BlockSpec((panel_count, vector_part, group, entry_part), lambda g: (0, 0, g, 0))],
        out_specs=pl.BlockSpec((group, panel_count * vector_part, entry_part), lambda g: (g, 0, 0)),
    )(panels)


def factor_inverse(gram_matrix):
    lower_factor = jnp.linalg.cholesky(gram_matrix)
    identity = jnp.broadcast_to(
        jnp.eye(gram_matrix.shape[-1], dtype=gram_matrix.dtype), gram_matrix.shape
    )
    return lax.linalg.triangular_solve(lower_factor, identity, left_side=True, lower=True)


def send(block_major):
    return lax.all_to_all(block_major, ("lat", "mode"), split_axis=0, concat_axis=0, tiled=True)


def split_by_source(received):
    lat_count = lax.axis_size("lat")
    mode_count = lax.axis_size("mode")
    return received.reshape(lat_count, mode_count, received.shape[1], received.shape[2])


def arrange(received):
    by_source = split_by_source(received)
    lat_count, mode_count, vector_part, entry_part = by_source.shape
    whole = by_source.transpose(1, 2, 0, 3)
    return whole.reshape(mode_count * vector_part, 1, lat_count * entry_part)


def project(earlier, finished, vectors, block_len):
    count = vectors.shape[0]
    pieces = [piece.reshape(piece.shape[0], block_len) for piece in [earlier] + finished]
    residual, gram_matrix = project_call(pieces, vectors.reshape(count, block_len))
    inverse = factor_inverse(gram_matrix)
    fresh = jnp.dot(inverse, residual.astype(jnp.float32), precision=lax.Precision.HIGHEST)
    return fresh.astype(jnp.bfloat16).reshape(count, 1, block_len)


def per_device(earlier, panels, further):
    block_len = earlier.shape[2]
    panel_count = panels.shape[0]
    vector_part = panels.shape[1]
    outgoing = block_major(panels)
    panels_arrived = send(outgoing)
    further_arrived = send(further.transpose(1, 0, 2))
    finished = []
    for panel_index in range(panel_count):
        part = panels_arrived[:, panel_index * vector_part:(panel_index + 1) * vector_part]
        finished.append(project(earlier, finished, arrange(part), block_len))
    new_basis = jnp.stack(finished, 0)
    new_basis, finished, further_arrived = lax.optimization_barrier(
        (new_basis, finished, further_arrived)
    )
    further_blocks = arrange(further_arrived)
    products = []
    for basis_part in [earlier] + finished:
        products.append(
            jnp.einsum(
                "nbl,pbl->pbn", basis_part, further_blocks, preferred_element_type=jnp.float32
            )
            / block_len
        )
    coarse = jnp.concatenate(products, axis=2)
    return (new_basis, coarse)


def solution(mesh):
    return jax.shard_map(
        per_device,
        mesh=mesh,
        in_specs=(
            P(None, ("lat", "mode"), None),
            P(None, "mode", None, "lat"),
            P("mode", None, "lat"),
        ),
        out_specs=(P(None, None, ("lat", "mode"), None), P(None, ("lat", "mode"), None)),
        check_vma=False,
    )
```

```python
import functools

import jax
import jax.numpy as jnp
from jax import lax
from jax.experimental import pallas as pl
from jax.experimental.pallas import tpu as pltpu
from jax.sharding import PartitionSpec as P

NT = (((1,), (1,)), ((), ()))


def project_kernel(*refs, piece_count, block_len):
    basis_refs = refs[:piece_count]
    vectors_ref, residual_ref, gram_ref = refs[piece_count:]
    vectors = vectors_ref[...]
    removed = None
    for basis_ref in basis_refs:
        basis = basis_ref[...]
        coeffs_t = lax.dot_general(vectors, basis, NT, preferred_element_type=jnp.float32)
        coeffs_t = (coeffs_t / block_len).astype(jnp.bfloat16)
        term = jnp.dot(coeffs_t, basis, preferred_element_type=jnp.float32)
        removed = term if removed is None else removed + term
    residual = (vectors.astype(jnp.float32) - removed).astype(jnp.bfloat16)
    residual_ref[...] = residual
    gram_ref[...] = lax.dot_general(residual, residual, NT, preferred_element_type=jnp.float32) / block_len


def project_call(pieces, vectors):
    count, block_len = vectors.shape
    rows = sum(p.shape[0] for p in pieces)
    spec = pl.BlockSpec(memory_space=pltpu.MemorySpace.VMEM)
    return pl.pallas_call(
        functools.partial(project_kernel, piece_count=len(pieces), block_len=block_len),
        out_shape=(
            jax.ShapeDtypeStruct((count, block_len), jnp.bfloat16),
            jax.ShapeDtypeStruct((count, count), jnp.float32),
        ),
        in_specs=[spec] * (len(pieces) + 1),
        out_specs=(spec, spec),
        compiler_params=pltpu.CompilerParams(vmem_limit_bytes=48 * 1024 * 1024),
        cost_estimate=pl.CostEstimate(
            flops=4 * rows * count * block_len + 2 * count * count * block_len,
            transcendentals=0,
            bytes_accessed=2 * block_len * (rows + 2 * count) + 4 * count * count,
        ),
    )(*pieces, vectors)


def block_major_kernel(panels_ref, out_ref):
    rows = panels_ref[...]
    rows = rows.reshape(-1, rows.shape[2], rows.shape[3])
    out_ref[...] = jnp.swapaxes(rows, 0, 1)


def block_major(panels, group=16):
    panel_count, vector_part, block_count, entry_part = panels.shape
    group = min(group, block_count)
    return pl.pallas_call(
        block_major_kernel,
        grid=(block_count // group,),
        out_shape=jax.ShapeDtypeStruct(
            (block_count, panel_count * vector_part, entry_part), panels.dtype
        ),
        in_specs=[pl.BlockSpec((panel_count, vector_part, group, entry_part), lambda g: (0, 0, g, 0))],
        out_specs=pl.BlockSpec((group, panel_count * vector_part, entry_part), lambda g: (g, 0, 0)),
    )(panels)


def by_vector_kernel(received_ref, out_ref, *, lat_count, mode_count, entry_part):
    for lat_index in range(lat_count):
        rows = received_ref[lat_index * mode_count:(lat_index + 1) * mode_count]
        out_ref[:, lat_index * entry_part:(lat_index + 1) * entry_part] = rows.reshape(-1, entry_part)


def by_vector(received):
    lat_count = lax.axis_size("lat")
    mode_count = lax.axis_size("mode")
    _, vector_part, entry_part = received.shape
    kernel = functools.partial(
        by_vector_kernel, lat_count=lat_count, mode_count=mode_count, entry_part=entry_part
    )
    return pl.pallas_call(
        kernel,
        out_shape=jax.ShapeDtypeStruct(
            (mode_count * vector_part, lat_count * entry_part), received.dtype
        ),
    )(received)


def factor_inverse(gram_matrix):
    lower_factor = jnp.linalg.cholesky(gram_matrix)
    identity = jnp.broadcast_to(
        jnp.eye(gram_matrix.shape[-1], dtype=gram_matrix.dtype), gram_matrix.shape
    )
    return lax.linalg.triangular_solve(lower_factor, identity, left_side=True, lower=True)


def send(block_major):
    return lax.all_to_all(block_major, ("lat", "mode"), split_axis=0, concat_axis=0, tiled=True)


def split_by_source(received):
    lat_count = lax.axis_size("lat")
    mode_count = lax.axis_size("mode")
    return received.reshape(lat_count, mode_count, received.shape[1], received.shape[2])


def arrange(received):
    by_source = split_by_source(received)
    lat_count, mode_count, vector_part, entry_part = by_source.shape
    whole = by_source.transpose(1, 2, 0, 3)
    return whole.reshape(mode_count * vector_part, 1, lat_count * entry_part)


def project(earlier, finished, vectors, block_len):
    count = vectors.shape[0]
    pieces = [piece.reshape(piece.shape[0], block_len) for piece in [earlier] + finished]
    residual, gram_matrix = project_call(pieces, vectors.reshape(count, block_len))
    inverse = factor_inverse(gram_matrix)
    fresh = jnp.dot(inverse, residual.astype(jnp.float32), precision=lax.Precision.HIGHEST)
    return fresh.astype(jnp.bfloat16).reshape(count, 1, block_len)


def per_device(earlier, panels, further):
    block_len = earlier.shape[2]
    panel_count = panels.shape[0]
    vector_part = panels.shape[1]
    outgoing = block_major(panels)
    panels_arrived = send(outgoing)
    further_arrived = send(further.transpose(1, 0, 2))
    finished = []
    for panel_index in range(panel_count):
        part = panels_arrived[:, panel_index * vector_part:(panel_index + 1) * vector_part]
        finished.append(project(earlier, finished, arrange(part), block_len))
    new_basis = jnp.stack(finished, 0)
    new_basis, finished, further_arrived = lax.optimization_barrier(
        (new_basis, finished, further_arrived)
    )
    further_blocks = by_vector(further_arrived)[:, None, :]
    products = []
    for basis_part in [earlier] + finished:
        products.append(
            jnp.einsum(
                "nbl,pbl->pbn", basis_part, further_blocks, preferred_element_type=jnp.float32
            )
            / block_len
        )
    coarse = jnp.concatenate(products, axis=2)
    return (new_basis, coarse)


def solution(mesh):
    return jax.shard_map(
        per_device,
        mesh=mesh,
        in_specs=(
            P(None, ("lat", "mode"), None),
            P(None, "mode", None, "lat"),
            P("mode", None, "lat"),
        ),
        out_specs=(P(None, None, ("lat", "mode"), None), P(None, ("lat", "mode"), None)),
        check_vma=False,
    )
```

```python
import functools

import jax
import jax.numpy as jnp
from jax import lax
from jax.experimental import pallas as pl
from jax.experimental.pallas import tpu as pltpu
from jax.sharding import PartitionSpec as P

NT = (((1,), (1,)), ((), ()))


def project_kernel(*refs, piece_count, block_len):
    basis_refs = refs[:piece_count]
    vectors_ref, residual_ref, gram_ref = refs[piece_count:]
    vectors = vectors_ref[...]
    removed = None
    for basis_ref in basis_refs:
        basis = basis_ref[...]
        coeffs_t = lax.dot_general(vectors, basis, NT, preferred_element_type=jnp.float32)
        coeffs_t = (coeffs_t / block_len).astype(jnp.bfloat16)
        term = jnp.dot(coeffs_t, basis, preferred_element_type=jnp.float32)
        removed = term if removed is None else removed + term
    residual = (vectors.astype(jnp.float32) - removed).astype(jnp.bfloat16)
    residual_ref[...] = residual
    gram_ref[...] = lax.dot_general(residual, residual, NT, preferred_element_type=jnp.float32) / block_len


def project_call(pieces, vectors):
    count, block_len = vectors.shape
    rows = sum(p.shape[0] for p in pieces)
    spec = pl.BlockSpec(memory_space=pltpu.MemorySpace.VMEM)
    return pl.pallas_call(
        functools.partial(project_kernel, piece_count=len(pieces), block_len=block_len),
        out_shape=(
            jax.ShapeDtypeStruct((count, block_len), jnp.bfloat16),
            jax.ShapeDtypeStruct((count, count), jnp.float32),
        ),
        in_specs=[spec] * (len(pieces) + 1),
        out_specs=(spec, spec),
        compiler_params=pltpu.CompilerParams(vmem_limit_bytes=48 * 1024 * 1024),
        cost_estimate=pl.CostEstimate(
            flops=4 * rows * count * block_len + 2 * count * count * block_len,
            transcendentals=0,
            bytes_accessed=2 * block_len * (rows + 2 * count) + 4 * count * count,
        ),
    )(*pieces, vectors)


def block_major_kernel(panels_ref, out_ref):
    rows = panels_ref[...]
    rows = rows.reshape(-1, rows.shape[2], rows.shape[3])
    out_ref[...] = jnp.swapaxes(rows, 0, 1)


def block_major(panels, group=16):
    panel_count, vector_part, block_count, entry_part = panels.shape
    group = min(group, block_count)
    return pl.pallas_call(
        block_major_kernel,
        grid=(block_count // group,),
        out_shape=jax.ShapeDtypeStruct(
            (block_count, panel_count * vector_part, entry_part), panels.dtype
        ),
        in_specs=[pl.BlockSpec((panel_count, vector_part, group, entry_part), lambda g: (0, 0, g, 0))],
        out_specs=pl.BlockSpec((group, panel_count * vector_part, entry_part), lambda g: (g, 0, 0)),
    )(panels)


def factor_inverse(gram_matrix):
    lower_factor = jnp.linalg.cholesky(gram_matrix)
    identity = jnp.broadcast_to(
        jnp.eye(gram_matrix.shape[-1], dtype=gram_matrix.dtype), gram_matrix.shape
    )
    return lax.linalg.triangular_solve(lower_factor, identity, left_side=True, lower=True)


def send(block_major):
    return lax.all_to_all(block_major, ("lat", "mode"), split_axis=0, concat_axis=0, tiled=True)


def split_by_source(received):
    lat_count = lax.axis_size("lat")
    mode_count = lax.axis_size("mode")
    return received.reshape(lat_count, mode_count, received.shape[1], received.shape[2])


def arrange(received):
    by_source = split_by_source(received)
    lat_count, mode_count, vector_part, entry_part = by_source.shape
    whole = by_source.transpose(1, 2, 0, 3)
    return whole.reshape(mode_count * vector_part, 1, lat_count * entry_part)


def project(earlier, finished, vectors, block_len):
    count = vectors.shape[0]
    pieces = [piece.reshape(piece.shape[0], block_len) for piece in [earlier] + finished]
    residual, gram_matrix = project_call(pieces, vectors.reshape(count, block_len))
    inverse = factor_inverse(gram_matrix)
    fresh = jnp.dot(inverse, residual.astype(jnp.float32), precision=lax.Precision.HIGHEST)
    return fresh.astype(jnp.bfloat16).reshape(count, 1, block_len)


def per_device(earlier, panels, further):
    block_len = earlier.shape[2]
    panel_count = panels.shape[0]
    vector_part = panels.shape[1]
    outgoing = block_major(panels)
    panels_arrived = send(outgoing)
    further_arrived = send(further.transpose(1, 0, 2))
    finished = []
    for panel_index in range(panel_count):
        part = panels_arrived[:, panel_index * vector_part:(panel_index + 1) * vector_part]
        finished.append(project(earlier, finished, arrange(part), block_len))
    new_basis = jnp.stack(finished, 0)
    new_basis, finished, further_arrived = lax.optimization_barrier(
        (new_basis, finished, further_arrived)
    )
    further_blocks = arrange(further_arrived)
    earlier_part = jnp.einsum(
        "nbl,pbl->pbn", earlier, further_blocks, preferred_element_type=jnp.float32
    )
    new_part = jnp.einsum(
        "knbl,pbl->pbkn", new_basis, further_blocks, preferred_element_type=jnp.float32
    )
    new_part = new_part.reshape(new_part.shape[0], new_part.shape[1], -1)
    products = [earlier_part / block_len, new_part / block_len]
    coarse = jnp.concatenate(products, axis=2)
    return (new_basis, coarse)


def solution(mesh):
    return jax.shard_map(
        per_device,
        mesh=mesh,
        in_specs=(
            P(None, ("lat", "mode"), None),
            P(None, "mode", None, "lat"),
            P("mode", None, "lat"),
        ),
        out_specs=(P(None, None, ("lat", "mode"), None), P(None, ("lat", "mode"), None)),
        check_vma=False,
    )
```

```python
import functools

import jax
import jax.numpy as jnp
from jax import lax
from jax.experimental import pallas as pl
from jax.experimental.pallas import tpu as pltpu
from jax.sharding import PartitionSpec as P

NT = (((1,), (1,)), ((), ()))


def project_kernel(*refs, piece_count, block_len):
    basis_refs = refs[:piece_count]
    vectors_ref, residual_ref, gram_ref = refs[piece_count:]
    vectors = vectors_ref[...]
    removed = None
    for basis_ref in basis_refs:
        basis = basis_ref[...]
        coeffs_t = lax.dot_general(vectors, basis, NT, preferred_element_type=jnp.float32)
        coeffs_t = (coeffs_t / block_len).astype(jnp.bfloat16)
        term = jnp.dot(coeffs_t, basis, preferred_element_type=jnp.float32)
        removed = term if removed is None else removed + term
    residual = (vectors.astype(jnp.float32) - removed).astype(jnp.bfloat16)
    residual_ref[...] = residual
    gram_ref[...] = lax.dot_general(residual, residual, NT, preferred_element_type=jnp.float32) / block_len


def project_call(pieces, vectors):
    count, block_len = vectors.shape
    rows = sum(p.shape[0] for p in pieces)
    spec = pl.BlockSpec(memory_space=pltpu.MemorySpace.VMEM)
    return pl.pallas_call(
        functools.partial(project_kernel, piece_count=len(pieces), block_len=block_len),
        out_shape=(
            jax.ShapeDtypeStruct((count, block_len), jnp.bfloat16),
            jax.ShapeDtypeStruct((count, count), jnp.float32),
        ),
        in_specs=[spec] * (len(pieces) + 1),
        out_specs=(spec, spec),
        compiler_params=pltpu.CompilerParams(vmem_limit_bytes=48 * 1024 * 1024),
        cost_estimate=pl.CostEstimate(
            flops=4 * rows * count * block_len + 2 * count * count * block_len,
            transcendentals=0,
            bytes_accessed=2 * block_len * (rows + 2 * count) + 4 * count * count,
        ),
    )(*pieces, vectors)


def block_major_kernel(panels_ref, out_ref):
    rows = panels_ref[...]
    rows = rows.reshape(-1, rows.shape[2], rows.shape[3])
    out_ref[...] = jnp.swapaxes(rows, 0, 1)


def block_major(panels, group=16):
    panel_count, vector_part, block_count, entry_part = panels.shape
    group = min(group, block_count)
    return pl.pallas_call(
        block_major_kernel,
        grid=(block_count // group,),
        out_shape=jax.ShapeDtypeStruct(
            (block_count, panel_count * vector_part, entry_part), panels.dtype
        ),
        in_specs=[pl.BlockSpec((panel_count, vector_part, group, entry_part), lambda g: (0, 0, g, 0))],
        out_specs=pl.BlockSpec((group, panel_count * vector_part, entry_part), lambda g: (g, 0, 0)),
    )(panels)


def coarse_kernel(received_ref, earlier_ref, fresh_ref, earlier_out, fresh_out, vectors, *,
                  lat_count, mode_count, entry_part, block_len):
    for lat_index in range(lat_count):
        rows = received_ref[lat_index * mode_count:(lat_index + 1) * mode_count]
        vectors[:, lat_index * entry_part:(lat_index + 1) * entry_part] = rows.reshape(-1, entry_part)
    further_rows = vectors[...]
    earlier_out[...] = lax.dot_general(
        further_rows, earlier_ref[...], NT, preferred_element_type=jnp.float32) / block_len
    fresh_out[...] = lax.dot_general(
        further_rows, fresh_ref[...], NT, preferred_element_type=jnp.float32) / block_len


def coarse_call(received, earlier_rows, fresh_rows, lat_count, mode_count):
    _, vector_part, entry_part = received.shape
    count = mode_count * vector_part
    block_len = lat_count * entry_part
    kernel = functools.partial(coarse_kernel, lat_count=lat_count, mode_count=mode_count,
                               entry_part=entry_part, block_len=block_len)
    return pl.pallas_call(
        kernel,
        out_shape=(
            jax.ShapeDtypeStruct((count, earlier_rows.shape[0]), jnp.float32),
            jax.ShapeDtypeStruct((count, fresh_rows.shape[0]), jnp.float32),
        ),
        scratch_shapes=[pltpu.VMEM((count, block_len), received.dtype)],
        compiler_params=pltpu.CompilerParams(vmem_limit_bytes=48 * 1024 * 1024),
    )(received, earlier_rows, fresh_rows)


def factor_inverse(gram_matrix):
    lower_factor = jnp.linalg.cholesky(gram_matrix)
    identity = jnp.broadcast_to(
        jnp.eye(gram_matrix.shape[-1], dtype=gram_matrix.dtype), gram_matrix.shape
    )
    return lax.linalg.triangular_solve(lower_factor, identity, left_side=True, lower=True)


def send(block_major):
    return lax.all_to_all(block_major, ("lat", "mode"), split_axis=0, concat_axis=0, tiled=True)


def split_by_source(received):
    lat_count = lax.axis_size("lat")
    mode_count = lax.axis_size("mode")
    return received.reshape(lat_count, mode_count, received.shape[1], received.shape[2])


def arrange(received):
    by_source = split_by_source(received)
    lat_count, mode_count, vector_part, entry_part = by_source.shape
    whole = by_source.transpose(1, 2, 0, 3)
    return whole.reshape(mode_count * vector_part, 1, lat_count * entry_part)


def project(earlier, finished, vectors, block_len):
    count = vectors.shape[0]
    pieces = [piece.reshape(piece.shape[0], block_len) for piece in [earlier] + finished]
    residual, gram_matrix = project_call(pieces, vectors.reshape(count, block_len))
    inverse = factor_inverse(gram_matrix)
    fresh = jnp.dot(inverse, residual.astype(jnp.float32), precision=lax.Precision.HIGHEST)
    return fresh.astype(jnp.bfloat16).reshape(count, 1, block_len)


def per_device(earlier, panels, further):
    block_len = earlier.shape[2]
    panel_count = panels.shape[0]
    vector_part = panels.shape[1]
    outgoing = block_major(panels)
    panels_arrived = send(outgoing)
    further_arrived = send(further.transpose(1, 0, 2))
    finished = []
    for panel_index in range(panel_count):
        part = panels_arrived[:, panel_index * vector_part:(panel_index + 1) * vector_part]
        finished.append(project(earlier, finished, arrange(part), block_len))
    new_basis = jnp.stack(finished, 0)
    new_basis, finished, further_arrived = lax.optimization_barrier(
        (new_basis, finished, further_arrived)
    )
    lat_count = lax.axis_size("lat")
    mode_count = lax.axis_size("mode")
    earlier_part, fresh_part = coarse_call(
        further_arrived,
        earlier.reshape(earlier.shape[0], block_len),
        new_basis.reshape(-1, block_len),
        lat_count,
        mode_count,
    )
    coarse = jnp.concatenate([earlier_part, fresh_part], axis=1)[:, None, :]
    return (new_basis, coarse)


def solution(mesh):
    return jax.shard_map(
        per_device,
        mesh=mesh,
        in_specs=(
            P(None, ("lat", "mode"), None),
            P(None, "mode", None, "lat"),
            P("mode", None, "lat"),
        ),
        out_specs=(P(None, None, ("lat", "mode"), None), P(None, ("lat", "mode"), None)),
        check_vma=False,
    )
```

```python
import functools

import jax
import jax.numpy as jnp
from jax import lax
from jax.experimental import pallas as pl
from jax.experimental.pallas import tpu as pltpu
from jax.sharding import PartitionSpec as P

NT = (((1,), (1,)), ((), ()))


def project_kernel(*refs, piece_count, block_len):
    basis_refs = refs[:piece_count]
    vectors_ref, residual_ref, gram_ref = refs[piece_count:]
    vectors = vectors_ref[...]
    removed = None
    for basis_ref in basis_refs:
        basis = basis_ref[...]
        coeffs_t = lax.dot_general(vectors, basis, NT, preferred_element_type=jnp.float32)
        coeffs_t = (coeffs_t / block_len).astype(jnp.bfloat16)
        term = jnp.dot(coeffs_t, basis, preferred_element_type=jnp.float32)
        removed = term if removed is None else removed + term
    residual = (vectors.astype(jnp.float32) - removed).astype(jnp.bfloat16)
    residual_ref[...] = residual
    gram_ref[...] = lax.dot_general(residual, residual, NT, preferred_element_type=jnp.float32) / block_len


def project_call(pieces, vectors):
    count, block_len = vectors.shape
    rows = sum(p.shape[0] for p in pieces)
    spec = pl.BlockSpec(memory_space=pltpu.MemorySpace.VMEM)
    return pl.pallas_call(
        functools.partial(project_kernel, piece_count=len(pieces), block_len=block_len),
        out_shape=(
            jax.ShapeDtypeStruct((count, block_len), jnp.bfloat16),
            jax.ShapeDtypeStruct((count, count), jnp.float32),
        ),
        in_specs=[spec] * (len(pieces) + 1),
        out_specs=(spec, spec),
        compiler_params=pltpu.CompilerParams(vmem_limit_bytes=48 * 1024 * 1024),
        cost_estimate=pl.CostEstimate(
            flops=4 * rows * count * block_len + 2 * count * count * block_len,
            transcendentals=0,
            bytes_accessed=2 * block_len * (rows + 2 * count) + 4 * count * count,
        ),
    )(*pieces, vectors)


def block_major_kernel(panels_ref, out_ref):
    rows = panels_ref[...]
    rows = rows.reshape(-1, rows.shape[2], rows.shape[3])
    out_ref[...] = jnp.swapaxes(rows, 0, 1)


def block_major(panels, group=16):
    panel_count, vector_part, block_count, entry_part = panels.shape
    group = min(group, block_count)
    return pl.pallas_call(
        block_major_kernel,
        grid=(block_count // group,),
        out_shape=jax.ShapeDtypeStruct(
            (block_count, panel_count * vector_part, entry_part), panels.dtype
        ),
        in_specs=[pl.BlockSpec((panel_count, vector_part, group, entry_part), lambda g: (0, 0, g, 0))],
        out_specs=pl.BlockSpec((group, panel_count * vector_part, entry_part), lambda g: (g, 0, 0)),
    )(panels)


def coarse_kernel(received_ref, earlier_ref, fresh_ref, out_ref, vectors, *,
                  lat_count, mode_count, entry_part, block_len):
    for lat_index in range(lat_count):
        rows = received_ref[lat_index * mode_count:(lat_index + 1) * mode_count]
        vectors[:, lat_index * entry_part:(lat_index + 1) * entry_part] = rows.reshape(-1, entry_part)
    further_rows = vectors[...]
    earlier_count = earlier_ref.shape[0]
    out_ref[:, :, :earlier_count] = (lax.dot_general(
        further_rows, earlier_ref[...], NT, preferred_element_type=jnp.float32) / block_len)[:, None, :]
    out_ref[:, :, earlier_count:] = (lax.dot_general(
        further_rows, fresh_ref[...], NT, preferred_element_type=jnp.float32) / block_len)[:, None, :]


def coarse_call(received, earlier_rows, fresh_rows, lat_count, mode_count):
    _, vector_part, entry_part = received.shape
    count = mode_count * vector_part
    block_len = lat_count * entry_part
    kernel = functools.partial(coarse_kernel, lat_count=lat_count, mode_count=mode_count,
                               entry_part=entry_part, block_len=block_len)
    return pl.pallas_call(
        kernel,
        out_shape=jax.ShapeDtypeStruct(
            (count, 1, earlier_rows.shape[0] + fresh_rows.shape[0]), jnp.float32
        ),
        scratch_shapes=[pltpu.VMEM((count, block_len), received.dtype)],
        compiler_params=pltpu.CompilerParams(vmem_limit_bytes=48 * 1024 * 1024),
    )(received, earlier_rows, fresh_rows)


def factor_inverse(gram_matrix):
    lower_factor = jnp.linalg.cholesky(gram_matrix)
    identity = jnp.broadcast_to(
        jnp.eye(gram_matrix.shape[-1], dtype=gram_matrix.dtype), gram_matrix.shape
    )
    return lax.linalg.triangular_solve(lower_factor, identity, left_side=True, lower=True)


def send(block_major):
    return lax.all_to_all(block_major, ("lat", "mode"), split_axis=0, concat_axis=0, tiled=True)


def split_by_source(received):
    lat_count = lax.axis_size("lat")
    mode_count = lax.axis_size("mode")
    return received.reshape(lat_count, mode_count, received.shape[1], received.shape[2])


def arrange(received):
    by_source = split_by_source(received)
    lat_count, mode_count, vector_part, entry_part = by_source.shape
    whole = by_source.transpose(1, 2, 0, 3)
    return whole.reshape(mode_count * vector_part, 1, lat_count * entry_part)


def project(earlier, finished, vectors, block_len):
    count = vectors.shape[0]
    pieces = [piece.reshape(piece.shape[0], block_len) for piece in [earlier] + finished]
    residual, gram_matrix = project_call(pieces, vectors.reshape(count, block_len))
    inverse = factor_inverse(gram_matrix)
    fresh = jnp.dot(inverse, residual.astype(jnp.float32), precision=lax.Precision.HIGHEST)
    return fresh.astype(jnp.bfloat16).reshape(count, 1, block_len)


def per_device(earlier, panels, further):
    block_len = earlier.shape[2]
    panel_count = panels.shape[0]
    vector_part = panels.shape[1]
    outgoing = block_major(panels)
    panels_arrived = send(outgoing)
    further_arrived = send(further.transpose(1, 0, 2))
    finished = []
    for panel_index in range(panel_count):
        part = panels_arrived[:, panel_index * vector_part:(panel_index + 1) * vector_part]
        finished.append(project(earlier, finished, arrange(part), block_len))
    new_basis = jnp.stack(finished, 0)
    new_basis, finished, further_arrived = lax.optimization_barrier(
        (new_basis, finished, further_arrived)
    )
    lat_count = lax.axis_size("lat")
    mode_count = lax.axis_size("mode")
    coarse = coarse_call(
        further_arrived,
        earlier.reshape(earlier.shape[0], block_len),
        new_basis.reshape(-1, block_len),
        lat_count,
        mode_count,
    )
    return (new_basis, coarse)


def solution(mesh):
    return jax.shard_map(
        per_device,
        mesh=mesh,
        in_specs=(
            P(None, ("lat", "mode"), None),
            P(None, "mode", None, "lat"),
            P("mode", None, "lat"),
        ),
        out_specs=(P(None, None, ("lat", "mode"), None), P(None, ("lat", "mode"), None)),
        check_vma=False,
    )
```

```python
import functools

import jax
import jax.numpy as jnp
from jax import lax
from jax.experimental import pallas as pl
from jax.experimental.pallas import tpu as pltpu
from jax.sharding import PartitionSpec as P

NT = (((1,), (1,)), ((), ()))


def project_kernel(*refs, piece_count, block_len):
    basis_refs = refs[:piece_count]
    vectors_ref, residual_ref, gram_ref = refs[piece_count:]
    vectors = vectors_ref[...]
    removed = None
    for basis_ref in basis_refs:
        basis = basis_ref[...]
        coeffs_t = lax.dot_general(vectors, basis, NT, preferred_element_type=jnp.float32)
        coeffs_t = (coeffs_t / block_len).astype(jnp.bfloat16)
        term = jnp.dot(coeffs_t, basis, preferred_element_type=jnp.float32)
        removed = term if removed is None else removed + term
    residual = (vectors.astype(jnp.float32) - removed).astype(jnp.bfloat16)
    residual_ref[...] = residual
    gram_ref[...] = lax.dot_general(residual, residual, NT, preferred_element_type=jnp.float32) / block_len


def project_call(pieces, vectors):
    count, block_len = vectors.shape
    rows = sum(p.shape[0] for p in pieces)
    spec = pl.BlockSpec(memory_space=pltpu.MemorySpace.VMEM)
    return pl.pallas_call(
        functools.partial(project_kernel, piece_count=len(pieces), block_len=block_len),
        out_shape=(
            jax.ShapeDtypeStruct((count, block_len), jnp.bfloat16),
            jax.ShapeDtypeStruct((count, count), jnp.float32),
        ),
        in_specs=[spec] * (len(pieces) + 1),
        out_specs=(spec, spec),
        compiler_params=pltpu.CompilerParams(vmem_limit_bytes=48 * 1024 * 1024),
        cost_estimate=pl.CostEstimate(
            flops=4 * rows * count * block_len + 2 * count * count * block_len,
            transcendentals=0,
            bytes_accessed=2 * block_len * (rows + 2 * count) + 4 * count * count,
        ),
    )(*pieces, vectors)


def block_major_kernel(panels_ref, out_ref):
    rows = panels_ref[...]
    rows = rows.reshape(-1, rows.shape[2], rows.shape[3])
    out_ref[...] = jnp.swapaxes(rows, 0, 1)


def block_major(panels, group=16):
    panel_count, vector_part, block_count, entry_part = panels.shape
    group = min(group, block_count)
    return pl.pallas_call(
        block_major_kernel,
        grid=(block_count // group,),
        out_shape=jax.ShapeDtypeStruct(
            (block_count, panel_count * vector_part, entry_part), panels.dtype
        ),
        in_specs=[pl.BlockSpec((panel_count, vector_part, group, entry_part), lambda g: (0, 0, g, 0))],
        out_specs=pl.BlockSpec((group, panel_count * vector_part, entry_part), lambda g: (g, 0, 0)),
    )(panels)


def coarse_kernel(received_ref, earlier_ref, fresh_ref, earlier_out, fresh_out):
    @pl.when(pl.program_id(0) == 0)
    def _():
        earlier_out[...] = jnp.zeros_like(earlier_out)
        fresh_out[...] = jnp.zeros_like(fresh_out)

    rows = received_ref[...]
    further_rows = rows.reshape(-1, rows.shape[2])
    earlier_out[...] += lax.dot_general(
        further_rows, earlier_ref[...], NT, preferred_element_type=jnp.float32)
    fresh_out[...] += lax.dot_general(
        further_rows, fresh_ref[...], NT, preferred_element_type=jnp.float32)


def coarse_call(received, earlier_rows, fresh_rows, lat_count, mode_count):
    _, vector_part, entry_part = received.shape
    count = mode_count * vector_part
    earlier_count = earlier_rows.shape[0]
    fresh_count = fresh_rows.shape[0]
    return pl.pallas_call(
        coarse_kernel,
        grid=(lat_count,),
        out_shape=(
            jax.ShapeDtypeStruct((count, earlier_count), jnp.float32),
            jax.ShapeDtypeStruct((count, fresh_count), jnp.float32),
        ),
        in_specs=[
            pl.BlockSpec((mode_count, vector_part, entry_part), lambda l: (l, 0, 0)),
            pl.BlockSpec((earlier_count, entry_part), lambda l: (0, l)),
            pl.BlockSpec((fresh_count, entry_part), lambda l: (0, l)),
        ],
        out_specs=(
            pl.BlockSpec((count, earlier_count), lambda l: (0, 0)),
            pl.BlockSpec((count, fresh_count), lambda l: (0, 0)),
        ),
    )(received, earlier_rows, fresh_rows)


def factor_inverse(gram_matrix):
    lower_factor = jnp.linalg.cholesky(gram_matrix)
    identity = jnp.broadcast_to(
        jnp.eye(gram_matrix.shape[-1], dtype=gram_matrix.dtype), gram_matrix.shape
    )
    return lax.linalg.triangular_solve(lower_factor, identity, left_side=True, lower=True)


def send(block_major):
    return lax.all_to_all(block_major, ("lat", "mode"), split_axis=0, concat_axis=0, tiled=True)


def split_by_source(received):
    lat_count = lax.axis_size("lat")
    mode_count = lax.axis_size("mode")
    return received.reshape(lat_count, mode_count, received.shape[1], received.shape[2])


def arrange(received):
    by_source = split_by_source(received)
    lat_count, mode_count, vector_part, entry_part = by_source.shape
    whole = by_source.transpose(1, 2, 0, 3)
    return whole.reshape(mode_count * vector_part, 1, lat_count * entry_part)


def project(earlier, finished, vectors, block_len):
    count = vectors.shape[0]
    pieces = [piece.reshape(piece.shape[0], block_len) for piece in [earlier] + finished]
    residual, gram_matrix = project_call(pieces, vectors.reshape(count, block_len))
    inverse = factor_inverse(gram_matrix)
    fresh = jnp.dot(inverse, residual.astype(jnp.float32), precision=lax.Precision.HIGHEST)
    return fresh.astype(jnp.bfloat16).reshape(count, 1, block_len)


def per_device(earlier, panels, further):
    block_len = earlier.shape[2]
    panel_count = panels.shape[0]
    vector_part = panels.shape[1]
    outgoing = block_major(panels)
    panels_arrived = send(outgoing)
    further_arrived = send(further.transpose(1, 0, 2))
    finished = []
    for panel_index in range(panel_count):
        part = panels_arrived[:, panel_index * vector_part:(panel_index + 1) * vector_part]
        finished.append(project(earlier, finished, arrange(part), block_len))
    new_basis = jnp.stack(finished, 0)
    new_basis, finished, further_arrived = lax.optimization_barrier(
        (new_basis, finished, further_arrived)
    )
    lat_count = lax.axis_size("lat")
    mode_count = lax.axis_size("mode")
    earlier_part, fresh_part = coarse_call(
        further_arrived,
        earlier.reshape(earlier.shape[0], block_len),
        new_basis.reshape(-1, block_len),
        lat_count,
        mode_count,
    )
    coarse = (jnp.concatenate([earlier_part, fresh_part], axis=1) / block_len)[:, None, :]
    return (new_basis, coarse)


def solution(mesh):
    return jax.shard_map(
        per_device,
        mesh=mesh,
        in_specs=(
            P(None, ("lat", "mode"), None),
            P(None, "mode", None, "lat"),
            P("mode", None, "lat"),
        ),
        out_specs=(P(None, None, ("lat", "mode"), None), P(None, ("lat", "mode"), None)),
        check_vma=False,
    )
```

```python
import functools

import jax
import jax.numpy as jnp
from jax import lax
from jax.experimental import pallas as pl
from jax.experimental.pallas import tpu as pltpu
from jax.sharding import PartitionSpec as P

NT = (((1,), (1,)), ((), ()))


def project_kernel(*refs, piece_count, block_len):
    basis_refs = refs[:piece_count]
    vectors_ref, residual_ref, gram_ref = refs[piece_count:]
    vectors = vectors_ref[...]
    removed = None
    for basis_ref in basis_refs:
        basis = basis_ref[...]
        coeffs_t = lax.dot_general(vectors, basis, NT, preferred_element_type=jnp.float32)
        coeffs_t = (coeffs_t / block_len).astype(jnp.bfloat16)
        term = jnp.dot(coeffs_t, basis, preferred_element_type=jnp.float32)
        removed = term if removed is None else removed + term
    residual = (vectors.astype(jnp.float32) - removed).astype(jnp.bfloat16)
    residual_ref[...] = residual
    gram_ref[...] = lax.dot_general(residual, residual, NT, preferred_element_type=jnp.float32) / block_len


def project_call(pieces, vectors):
    count, block_len = vectors.shape
    rows = sum(p.shape[0] for p in pieces)
    spec = pl.BlockSpec(memory_space=pltpu.MemorySpace.VMEM)
    return pl.pallas_call(
        functools.partial(project_kernel, piece_count=len(pieces), block_len=block_len),
        out_shape=(
            jax.ShapeDtypeStruct((count, block_len), jnp.bfloat16),
            jax.ShapeDtypeStruct((count, count), jnp.float32),
        ),
        in_specs=[spec] * (len(pieces) + 1),
        out_specs=(spec, spec),
        compiler_params=pltpu.CompilerParams(vmem_limit_bytes=48 * 1024 * 1024),
        cost_estimate=pl.CostEstimate(
            flops=4 * rows * count * block_len + 2 * count * count * block_len,
            transcendentals=0,
            bytes_accessed=2 * block_len * (rows + 2 * count) + 4 * count * count,
        ),
    )(*pieces, vectors)


def block_major_kernel(panels_ref, out_ref):
    rows = panels_ref[...]
    rows = rows.reshape(-1, rows.shape[2], rows.shape[3])
    out_ref[...] = jnp.swapaxes(rows, 0, 1)


def block_major(panels, group=16):
    panel_count, vector_part, block_count, entry_part = panels.shape
    group = min(group, block_count)
    return pl.pallas_call(
        block_major_kernel,
        grid=(block_count // group,),
        out_shape=jax.ShapeDtypeStruct(
            (block_count, panel_count * vector_part, entry_part), panels.dtype
        ),
        in_specs=[pl.BlockSpec((panel_count, vector_part, group, entry_part), lambda g: (0, 0, g, 0))],
        out_specs=pl.BlockSpec((group, panel_count * vector_part, entry_part), lambda g: (g, 0, 0)),
    )(panels)


def coarse_kernel(received_ref, earlier_ref, fresh_ref, earlier_out, fresh_out, vectors, *,
                  lat_count, mode_count, entry_part):
    @pl.when(pl.program_id(0) == 0)
    def _():
        earlier_out[...] = jnp.zeros_like(earlier_out)
        fresh_out[...] = jnp.zeros_like(fresh_out)

    for lat_index in range(lat_count):
        rows = received_ref[lat_index * mode_count:(lat_index + 1) * mode_count]
        vectors[:, lat_index * entry_part:(lat_index + 1) * entry_part] = rows.reshape(-1, entry_part)
    further_rows = vectors[...]
    earlier_out[...] += lax.dot_general(
        further_rows, earlier_ref[...], NT, preferred_element_type=jnp.float32)
    fresh_out[...] += lax.dot_general(
        further_rows, fresh_ref[...], NT, preferred_element_type=jnp.float32)


def coarse_call(received, earlier_rows, fresh_rows, lat_count, mode_count, steps=2):
    _, vector_part, entry_part = received.shape
    count = mode_count * vector_part
    steps = steps if lat_count % steps == 0 else 1
    lat_step = lat_count // steps
    kernel = functools.partial(coarse_kernel, lat_count=lat_step, mode_count=mode_count,
                               entry_part=entry_part)
    earlier_count = earlier_rows.shape[0]
    fresh_count = fresh_rows.shape[0]
    return pl.pallas_call(
        kernel,
        grid=(steps,),
        out_shape=(
            jax.ShapeDtypeStruct((count, earlier_count), jnp.float32),
            jax.ShapeDtypeStruct((count, fresh_count), jnp.float32),
        ),
        in_specs=[
            pl.BlockSpec((lat_step * mode_count, vector_part, entry_part), lambda s: (s, 0, 0)),
            pl.BlockSpec((earlier_count, lat_step * entry_part), lambda s: (0, s)),
            pl.BlockSpec((fresh_count, lat_step * entry_part), lambda s: (0, s)),
        ],
        out_specs=(
            pl.BlockSpec((count, earlier_count), lambda s: (0, 0)),
            pl.BlockSpec((count, fresh_count), lambda s: (0, 0)),
        ),
        scratch_shapes=[pltpu.VMEM((count, lat_step * entry_part), received.dtype)],
        compiler_params=pltpu.CompilerParams(vmem_limit_bytes=48 * 1024 * 1024),
    )(received, earlier_rows, fresh_rows)


def factor_inverse(gram_matrix):
    lower_factor = jnp.linalg.cholesky(gram_matrix)
    identity = jnp.broadcast_to(
        jnp.eye(gram_matrix.shape[-1], dtype=gram_matrix.dtype), gram_matrix.shape
    )
    return lax.linalg.triangular_solve(lower_factor, identity, left_side=True, lower=True)


def send(block_major):
    return lax.all_to_all(block_major, ("lat", "mode"), split_axis=0, concat_axis=0, tiled=True)


def split_by_source(received):
    lat_count = lax.axis_size("lat")
    mode_count = lax.axis_size("mode")
    return received.reshape(lat_count, mode_count, received.shape[1], received.shape[2])


def arrange(received):
    by_source = split_by_source(received)
    lat_count, mode_count, vector_part, entry_part = by_source.shape
    whole = by_source.transpose(1, 2, 0, 3)
    return whole.reshape(mode_count * vector_part, 1, lat_count * entry_part)


def project(earlier, finished, vectors, block_len):
    count = vectors.shape[0]
    pieces = [piece.reshape(piece.shape[0], block_len) for piece in [earlier] + finished]
    residual, gram_matrix = project_call(pieces, vectors.reshape(count, block_len))
    inverse = factor_inverse(gram_matrix)
    fresh = jnp.dot(inverse, residual.astype(jnp.float32), precision=lax.Precision.HIGHEST)
    return fresh.astype(jnp.bfloat16).reshape(count, 1, block_len)


def per_device(earlier, panels, further):
    block_len = earlier.shape[2]
    panel_count = panels.shape[0]
    vector_part = panels.shape[1]
    outgoing = block_major(panels)
    panels_arrived = send(outgoing)
    further_arrived = send(further.transpose(1, 0, 2))
    finished = []
    for panel_index in range(panel_count):
        part = panels_arrived[:, panel_index * vector_part:(panel_index + 1) * vector_part]
        finished.append(project(earlier, finished, arrange(part), block_len))
    new_basis = jnp.stack(finished, 0)
    new_basis, finished, further_arrived = lax.optimization_barrier(
        (new_basis, finished, further_arrived)
    )
    lat_count = lax.axis_size("lat")
    mode_count = lax.axis_size("mode")
    earlier_part, fresh_part = coarse_call(
        further_arrived,
        earlier.reshape(earlier.shape[0], block_len),
        new_basis.reshape(-1, block_len),
        lat_count,
        mode_count,
    )
    coarse = (jnp.concatenate([earlier_part, fresh_part], axis=1) / block_len)[:, None, :]
    return (new_basis, coarse)


def solution(mesh):
    return jax.shard_map(
        per_device,
        mesh=mesh,
        in_specs=(
            P(None, ("lat", "mode"), None),
            P(None, "mode", None, "lat"),
            P("mode", None, "lat"),
        ),
        out_specs=(P(None, None, ("lat", "mode"), None), P(None, ("lat", "mode"), None)),
        check_vma=False,
    )
```

```python
import functools

import jax
import jax.numpy as jnp
from jax import lax
from jax.experimental import pallas as pl
from jax.experimental.pallas import tpu as pltpu
from jax.sharding import PartitionSpec as P

NT = (((1,), (1,)), ((), ()))


def project_kernel(*refs, piece_count, block_len):
    basis_refs = refs[:piece_count]
    vectors_ref, residual_ref, gram_ref = refs[piece_count:]
    vectors = vectors_ref[...]
    removed = None
    for basis_ref in basis_refs:
        basis = basis_ref[...]
        coeffs_t = lax.dot_general(vectors, basis, NT, preferred_element_type=jnp.float32)
        coeffs_t = (coeffs_t / block_len).astype(jnp.bfloat16)
        term = jnp.dot(coeffs_t, basis, preferred_element_type=jnp.float32)
        removed = term if removed is None else removed + term
    residual = (vectors.astype(jnp.float32) - removed).astype(jnp.bfloat16)
    residual_ref[...] = residual
    gram_ref[...] = lax.dot_general(residual, residual, NT, preferred_element_type=jnp.float32) / block_len


def project_call(pieces, vectors):
    count, block_len = vectors.shape
    rows = sum(p.shape[0] for p in pieces)
    spec = pl.BlockSpec(memory_space=pltpu.MemorySpace.VMEM)
    return pl.pallas_call(
        functools.partial(project_kernel, piece_count=len(pieces), block_len=block_len),
        out_shape=(
            jax.ShapeDtypeStruct((count, block_len), jnp.bfloat16),
            jax.ShapeDtypeStruct((count, count), jnp.float32),
        ),
        in_specs=[spec] * (len(pieces) + 1),
        out_specs=(spec, spec),
        compiler_params=pltpu.CompilerParams(vmem_limit_bytes=48 * 1024 * 1024),
        cost_estimate=pl.CostEstimate(
            flops=4 * rows * count * block_len + 2 * count * count * block_len,
            transcendentals=0,
            bytes_accessed=2 * block_len * (rows + 2 * count) + 4 * count * count,
        ),
    )(*pieces, vectors)


def block_major_kernel(panels_ref, out_ref):
    rows = panels_ref[...]
    rows = rows.reshape(-1, rows.shape[2], rows.shape[3])
    out_ref[...] = jnp.swapaxes(rows, 0, 1)


def block_major(panels, group=16):
    panel_count, vector_part, block_count, entry_part = panels.shape
    group = min(group, block_count)
    return pl.pallas_call(
        block_major_kernel,
        grid=(block_count // group,),
        out_shape=jax.ShapeDtypeStruct(
            (block_count, panel_count * vector_part, entry_part), panels.dtype
        ),
        in_specs=[pl.BlockSpec((panel_count, vector_part, group, entry_part), lambda g: (0, 0, g, 0))],
        out_specs=pl.BlockSpec((group, panel_count * vector_part, entry_part), lambda g: (g, 0, 0)),
    )(panels)


def coarse_kernel(received_ref, earlier_ref, fresh_ref, earlier_out, fresh_out, vectors, *,
                  lat_count, mode_count, entry_part):
    @pl.when(pl.program_id(0) == 0)
    def _():
        earlier_out[...] = jnp.zeros_like(earlier_out)
        fresh_out[...] = jnp.zeros_like(fresh_out)

    for lat_index in range(lat_count):
        rows = received_ref[lat_index * mode_count:(lat_index + 1) * mode_count]
        vectors[:, lat_index * entry_part:(lat_index + 1) * entry_part] = rows.reshape(-1, entry_part)
    further_rows = vectors[...]
    earlier_out[...] += lax.dot_general(
        further_rows, earlier_ref[...], NT, preferred_element_type=jnp.float32)
    fresh_out[...] += lax.dot_general(
        further_rows, fresh_ref[...], NT, preferred_element_type=jnp.float32)


def coarse_call(received, earlier_rows, fresh_rows, lat_count, mode_count, steps=4):
    _, vector_part, entry_part = received.shape
    count = mode_count * vector_part
    steps = steps if lat_count % steps == 0 else 1
    lat_step = lat_count // steps
    kernel = functools.partial(coarse_kernel, lat_count=lat_step, mode_count=mode_count,
                               entry_part=entry_part)
    earlier_count = earlier_rows.shape[0]
    fresh_count = fresh_rows.shape[0]
    return pl.pallas_call(
        kernel,
        grid=(steps,),
        out_shape=(
            jax.ShapeDtypeStruct((count, earlier_count), jnp.float32),
            jax.ShapeDtypeStruct((count, fresh_count), jnp.float32),
        ),
        in_specs=[
            pl.BlockSpec((lat_step * mode_count, vector_part, entry_part), lambda s: (s, 0, 0)),
            pl.BlockSpec((earlier_count, lat_step * entry_part), lambda s: (0, s)),
            pl.BlockSpec((fresh_count, lat_step * entry_part), lambda s: (0, s)),
        ],
        out_specs=(
            pl.BlockSpec((count, earlier_count), lambda s: (0, 0)),
            pl.BlockSpec((count, fresh_count), lambda s: (0, 0)),
        ),
        scratch_shapes=[pltpu.VMEM((count, lat_step * entry_part), received.dtype)],
        compiler_params=pltpu.CompilerParams(vmem_limit_bytes=48 * 1024 * 1024),
    )(received, earlier_rows, fresh_rows)


def factor_inverse(gram_matrix):
    lower_factor = jnp.linalg.cholesky(gram_matrix)
    identity = jnp.broadcast_to(
        jnp.eye(gram_matrix.shape[-1], dtype=gram_matrix.dtype), gram_matrix.shape
    )
    return lax.linalg.triangular_solve(lower_factor, identity, left_side=True, lower=True)


def send(block_major):
    return lax.all_to_all(block_major, ("lat", "mode"), split_axis=0, concat_axis=0, tiled=True)


def split_by_source(received):
    lat_count = lax.axis_size("lat")
    mode_count = lax.axis_size("mode")
    return received.reshape(lat_count, mode_count, received.shape[1], received.shape[2])


def arrange(received):
    by_source = split_by_source(received)
    lat_count, mode_count, vector_part, entry_part = by_source.shape
    whole = by_source.transpose(1, 2, 0, 3)
    return whole.reshape(mode_count * vector_part, 1, lat_count * entry_part)


def project(earlier, finished, vectors, block_len):
    count = vectors.shape[0]
    pieces = [piece.reshape(piece.shape[0], block_len) for piece in [earlier] + finished]
    residual, gram_matrix = project_call(pieces, vectors.reshape(count, block_len))
    inverse = factor_inverse(gram_matrix)
    fresh = jnp.dot(inverse, residual.astype(jnp.float32), precision=lax.Precision.HIGHEST)
    return fresh.astype(jnp.bfloat16).reshape(count, 1, block_len)


def per_device(earlier, panels, further):
    block_len = earlier.shape[2]
    panel_count = panels.shape[0]
    vector_part = panels.shape[1]
    outgoing = block_major(panels)
    panels_arrived = send(outgoing)
    further_arrived = send(further.transpose(1, 0, 2))
    finished = []
    for panel_index in range(panel_count):
        part = panels_arrived[:, panel_index * vector_part:(panel_index + 1) * vector_part]
        finished.append(project(earlier, finished, arrange(part), block_len))
    new_basis = jnp.stack(finished, 0)
    new_basis, finished, further_arrived = lax.optimization_barrier(
        (new_basis, finished, further_arrived)
    )
    lat_count = lax.axis_size("lat")
    mode_count = lax.axis_size("mode")
    earlier_part, fresh_part = coarse_call(
        further_arrived,
        earlier.reshape(earlier.shape[0], block_len),
        new_basis.reshape(-1, block_len),
        lat_count,
        mode_count,
    )
    coarse = (jnp.concatenate([earlier_part, fresh_part], axis=1) / block_len)[:, None, :]
    return (new_basis, coarse)


def solution(mesh):
    return jax.shard_map(
        per_device,
        mesh=mesh,
        in_specs=(
            P(None, ("lat", "mode"), None),
            P(None, "mode", None, "lat"),
            P("mode", None, "lat"),
        ),
        out_specs=(P(None, None, ("lat", "mode"), None), P(None, ("lat", "mode"), None)),
        check_vma=False,
    )
```
